512 devices in a mesh: sec: 2 (over core), lat: 8 (over y_hi, x), lon: 32 (over z, y_lo).
Axes of the slice: x: 4, y: 4 (y_hi: 2, y_lo: 2; y = y_hi * 2 + y_lo), z: 16, core: 2. Of those that a mesh axis runs over, the one named last changes fastest.
Arguments:
- state: float32 [2, 2, 60, 128, 4096], P('sec', None, None, 'lat', 'lon'), may hold values from -6 to 6
- zonal: float32 [2, 60, 128, 4096], P('sec', None, 'lat', 'lon'), may hold values from -0.45 to 0.45
- meridional: float32 [2, 60, 128, 4096], P('sec', None, 'lat', 'lon'), may hold values from -0.35 to 0.35
- mixing: float32 [2, 60, 128, 4096], P('sec', None, 'lat', 'lon'), may hold values from 0.005 to 0.05
- exchange_rate: float32 [2, 128, 4096], P('sec', 'lat', 'lon'), may hold values from 0.02 to 0.1
- sea_mask: int32 [2, 128, 4096], P('sec', 'lat', 'lon'), may hold values 0 or 1
- regrid_map: int32 [2, 4, 128, 4096], P('sec', None, 'lat', 'lon'), may hold values from 0 to 2047, as said below
Outputs:
- final_state: float32 [2, 2, 60, 128, 4096], P('sec', None, None, 'lat', 'lon')
- surface_flux: float32 [2, 2, 128, 4096], P('sec', None, 'lat', 'lon')
The draws below stay inside these ranges and needn't reach their ends.
Inputs may be any that keep to these rules, and one draw needn't show every extreme that they name: regrid_map[s, t, cell] is the local number of a cell of the same block, at most 2 rows and 3 columns away (columns wrapping inside the block, rows clamped to it); entry t = 0 names the cell's own position.
All inputs are finite; a program needn't handle non-finite values. No bound on the sum of `sea_mask` on one device may be relied on, other than what follows from the above.
Results may differ from the reference program's by a relative error of at most 0.00002.
Values sent between devices are 32-bit elements; how exact they have to be, the bound alone decides.
No kernel may reach another device: no remote copies, remote signals or barrier semaphores. Data moves between devices by JAX's collectives and lax.ppermute only.
A program may use at most 128 MiB of HBM per device.

```python
import math
import jax
import jax.numpy as jnp

LEV = 60
FIELDS = 2
TAPS = 4
SUB = 4
CLAT = 16
CLON = 128
NLAT = 128
NLON = 4096
N_LAT = 8
N_LON = 32


def draw_regrid_map(key, part):
    row_key = jax.random.fold_in(key, 11)
    col_key = jax.random.fold_in(key, 23)
    shape = (2, TAPS, NLAT, NLON)
    local_row = (jnp.arange(NLAT, dtype=jnp.int32) % CLAT)[:, None]
    local_col = (jnp.arange(NLON, dtype=jnp.int32) % CLON)[None, :]
    row_step = jax.random.randint(row_key, shape, -2, 3, dtype=jnp.int32)
    col_step = jax.random.randint(col_key, shape, -3, 4, dtype=jnp.int32)
    rows = jnp.clip(local_row + row_step, 0, CLAT - 1)
    cols = (local_col + col_step) % CLON
    moved = rows * CLON + cols
    own = jnp.broadcast_to(local_row * CLON + local_col, shape)
    first = (jnp.arange(TAPS, dtype=jnp.int32) == 0)[None, :, None, None]
    return jnp.where(first, own, moved).astype(jnp.int32)


def place_ends(values, stream_key, least, high):
    longest = values.shape.index(max(values.shape))
    spots = []
    for shift in (0, 1):
        where = [jax.random.randint(jax.random.fold_in(stream_key, axis), (), 0, length) for axis, length in enumerate(values.shape)]
        where[longest] = (where[longest] + shift) % values.shape[longest]
        spots.append(tuple(where))
    return values.at[spots[0]].set(least).at[spots[1]].set(high)


def level_of(key, shape, shards, least, largest):
    level = 1.0
    for dim, shards_of in shards:
        steps = jax.random.uniform(jax.random.fold_in(jax.random.fold_in(key, 6), dim), (shards_of,), jnp.float32, least / len(shards), largest / len(shards))
        level = level * jnp.repeat(jnp.exp(steps), shape[dim] // shards_of).reshape((-1,) + (1,) * (len(shape) - 1 - dim))
    return level


def bell_draw(rng, dims, scale, reach, cuts=(), kind=jnp.bfloat16):
    values = scale * jax.random.normal(rng, dims, jnp.float32)
    if cuts:
        values = values * level_of(rng, dims, cuts, -0.22, 0.18)
    return jnp.clip(values, -reach, reach).astype(kind)


def setup_inputs(seed: int = 0) -> dict:
    keys = jax.random.split(jax.random.key(seed), 8)
    state = bell_draw(keys[0], (2, FIELDS, LEV, NLAT, NLON), 1.0, 6.0, ((0, 2), (3, 8), (4, 32)), jnp.float32)
    zonal = jnp.clip(jax.random.uniform(keys[1], (2, LEV, NLAT, NLON), jnp.float32, -0.45, 0.45) * level_of(keys[1], (2, LEV, NLAT, NLON), ((0, 2), (2, 8), (3, 32)), -0.4, 0.0), -0.45, 0.45)
    meridional = jnp.clip(jax.random.uniform(keys[2], (2, LEV, NLAT, NLON), jnp.float32, -0.35, 0.35) * level_of(keys[2], (2, LEV, NLAT, NLON), ((0, 2), (2, 8), (3, 32)), -0.4, 0.0), -0.35, 0.35)
    mixing = jnp.clip(jnp.exp(math.log(0.05) - 2.3025851 * jax.random.uniform(keys[3], (2, LEV, NLAT, NLON), jnp.float32) ** level_of(keys[3], (2, LEV, NLAT, NLON), ((0, 2), (2, 8), (3, 32)), -0.2, 0.2)), 0.005, 0.05)
    exchange_rate = jnp.clip(jnp.exp(math.log(0.1) - 1.609438 * jax.random.uniform(keys[4], (2, NLAT, NLON), jnp.float32) ** level_of(keys[4], (2, NLAT, NLON), ((0, 2), (1, 8), (2, 32)), -0.2, 0.2)), 0.02, 0.1)
    sea_mask = place_ends((jax.random.randint(keys[5], (2, NLAT, NLON), 0, 10) < 7).astype(jnp.int32), jax.random.fold_in(keys[5], 1), 0, 1)
    regrid_map = draw_regrid_map(jax.random.fold_in(keys[7], 71), 0)
    return dict(state=state, zonal=zonal, meridional=meridional, mixing=mixing, exchange_rate=exchange_rate, sea_mask=sea_mask, regrid_map=regrid_map)


def regrid(partner_surf, table):
    fields = partner_surf.shape[0]
    blocks = partner_surf.reshape(fields, N_LAT, CLAT, N_LON, CLON).transpose(0, 1, 3, 2, 4).reshape(fields, N_LAT, N_LON, CLAT * CLON)
    tables = table.reshape(TAPS, N_LAT, CLAT, N_LON, CLON).transpose(0, 1, 3, 2, 4).reshape(TAPS, N_LAT, N_LON, CLAT * CLON)
    total = jnp.zeros(blocks.shape, jnp.float32)
    for tap in range(TAPS):
        picks = jnp.broadcast_to(tables[tap][None], blocks.shape).astype(jnp.int32)
        total = total + jnp.take_along_axis(blocks, picks, axis=-1)
    mean = total / TAPS
    return mean.reshape(fields, N_LAT, N_LON, CLAT, CLON).transpose(0, 1, 3, 2, 4).reshape(fields, NLAT, NLON)


def advance(q, wet, zonal, meridional, mixing, flux):
    wet_w = jnp.roll(wet, 1, axis=1)
    wet_e = jnp.roll(wet, -1, axis=1)
    wet_s = jnp.pad(wet, ((1, 0), (0, 0)))[:-1]
    wet_n = jnp.pad(wet, ((0, 1), (0, 0)))[1:]
    q_w = jnp.roll(q, 1, axis=-1)
    q_e = jnp.roll(q, -1, axis=-1)
    q_s = jnp.roll(q, 1, axis=-2)
    q_n = jnp.roll(q, -1, axis=-2)
    horiz = (wet_w * jnp.maximum(zonal, 0.0)) * (q_w - q) + (wet_e * jnp.maximum(-zonal, 0.0)) * (q_e - q) + (wet_s * jnp.maximum(meridional, 0.0)) * (q_s - q) + (wet_n * jnp.maximum(-meridional, 0.0)) * (q_n - q)
    down = mixing[:-1] * (q[:, 1:] - q[:, :-1])
    vert = jnp.pad(down, ((0, 0), (0, 1), (0, 0), (0, 0))) - jnp.pad(down, ((0, 0), (1, 0), (0, 0), (0, 0)))
    updated = q + wet * (horiz + vert)
    return jnp.concatenate([updated[:, :1] + flux[:, None], updated[:, 1:]], axis=1)


def reference(state, zonal, meridional, mixing, exchange_rate, sea_mask, regrid_map):
    finals = []
    fluxes = []
    for section in range(2):
        partner = 1 - section
        sea = sea_mask[section].astype(jnp.float32)
        wet = sea if section == 1 else jnp.ones_like(sea)
        regridded = regrid(state[partner][:, 0], regrid_map[section])
        flux = (exchange_rate[section] * sea) * (regridded - state[section][:, 0])
        q = state[section]
        for step in range(SUB):
            q = advance(q, wet, zonal[section], meridional[section], mixing[section], flux)
        finals.append(q)
        fluxes.append(flux)
    return jnp.stack(finals), jnp.stack(fluxes)
```

```python
import jax
import jax.numpy as jnp
from jax import lax
from jax.sharding import PartitionSpec as P

TAPS = 4
SUB = 4
ROW_REACH = 2
COL_REACH = 3


def shifted(x, da, db):
    n_lat = lax.axis_size("lat")
    n_lon = lax.axis_size("lon")
    pairs = []
    for a in range(n_lat):
        for b in range(n_lon):
            src = a * n_lon + b
            dst = ((a + da) % n_lat) * n_lon + (b + db) % n_lon
            pairs.append((src, dst))
    flat = x.reshape(-1)
    return lax.ppermute(flat, ("lat", "lon"), pairs).reshape(x.shape)


def halo8(x, w):
    top = shifted(x[..., -w:, :], 1, 0)
    bottom = shifted(x[..., :w, :], -1, 0)
    left = shifted(x[..., :, -w:], 0, 1)
    right = shifted(x[..., :, :w], 0, -1)
    top_left = shifted(x[..., -w:, -w:], 1, 1)
    top_right = shifted(x[..., -w:, :w], 1, -1)
    bottom_left = shifted(x[..., :w, -w:], -1, 1)
    bottom_right = shifted(x[..., :w, :w], -1, -1)
    upper = jnp.concatenate([top_left, top, top_right], axis=-1)
    middle = jnp.concatenate([left, x, right], axis=-1)
    lower = jnp.concatenate([bottom_left, bottom, bottom_right], axis=-1)
    return jnp.concatenate([upper, middle, lower], axis=-2)


def regrid(partner, table):
    fields, rows, cols = partner.shape
    row = lax.broadcasted_iota(jnp.int32, (rows, cols), 0)
    col = lax.broadcasted_iota(jnp.int32, (rows, cols), 1)
    d_row = table // cols - row
    d_col = table % cols - col
    d_col = jnp.where(d_col > cols // 2, d_col - cols, d_col)
    d_col = jnp.where(d_col < -(cols // 2), d_col + cols, d_col)
    padded = jnp.concatenate(
        [jnp.repeat(partner[:, :1], ROW_REACH, axis=1), partner, jnp.repeat(partner[:, -1:], ROW_REACH, axis=1)],
        axis=1,
    )
    moved = {}
    for a in range(-ROW_REACH, ROW_REACH + 1):
        rows_a = padded[:, ROW_REACH + a : ROW_REACH + a + rows]
        for b in range(-COL_REACH, COL_REACH + 1):
            moved[a, b] = jnp.roll(rows_a, -b, axis=2)
    total = None
    for tap in range(TAPS):
        picked = moved[0, 0]
        for (a, b), values in moved.items():
            hit = jnp.logical_and(d_row[tap] == a, d_col[tap] == b)
            picked = jnp.where(hit[None], values, picked)
        total = picked if total is None else total + picked
    return total / TAPS


def advance(q, wet, zonal, meridional, mixing, flux):
    center = q[..., 1:-1, 1:-1]
    west = q[..., 1:-1, :-2]
    east = q[..., 1:-1, 2:]
    south = q[..., :-2, 1:-1]
    north = q[..., 2:, 1:-1]
    wet_c = wet[1:-1, 1:-1]
    wet_w = wet[1:-1, :-2]
    wet_e = wet[1:-1, 2:]
    wet_s = wet[:-2, 1:-1]
    wet_n = wet[2:, 1:-1]
    horiz = (
        (wet_w * jnp.maximum(zonal, 0.0)) * (west - center)
        + (wet_e * jnp.maximum(-zonal, 0.0)) * (east - center)
        + (wet_s * jnp.maximum(meridional, 0.0)) * (south - center)
        + (wet_n * jnp.maximum(-meridional, 0.0)) * (north - center)
    )
    down = mixing[:-1] * (center[:, 1:] - center[:, :-1])
    vert = jnp.pad(down, ((0, 0), (0, 1), (0, 0), (0, 0))) - jnp.pad(
        down, ((0, 0), (1, 0), (0, 0), (0, 0))
    )
    updated = center + wet_c * (horiz + vert)
    return jnp.concatenate([updated[:, :1] + flux[:, None], updated[:, 1:]], axis=1)


def crop(x, e):
    if e == 0:
        return x
    return x[..., e:-e, e:-e]


def shards(state, zonal, meridional, mixing, exchange_rate, sea_mask, regrid_map):
    tracers = state[0]
    fields, levels, rows, cols = tracers.shape
    section = lax.axis_index("sec")
    sea = sea_mask[0].astype(jnp.float32)
    wet = jnp.where(section == 1, sea, jnp.ones_like(sea))
    surface = tracers[:, 0]
    partner = lax.ppermute(surface, "sec", [(0, 1), (1, 0)])

    width = SUB
    stack = jnp.concatenate(
        [tracers.reshape(fields * levels, rows, cols), zonal[0], meridional[0], mixing[0], wet[None]], axis=0
    )
    ext = halo8(stack, width)
    n_q = fields * levels
    q = ext[:n_q].reshape(fields, levels, rows + 2 * width, cols + 2 * width)
    zonal_x = ext[n_q : n_q + levels]
    meridional_x = ext[n_q + levels : n_q + 2 * levels]
    mixing_x = ext[n_q + 2 * levels : n_q + 3 * levels]
    wet_x = ext[n_q + 3 * levels]
    row_block = lax.axis_index("lat")
    global_row = jnp.arange(rows + 2 * width, dtype=jnp.int32) + row_block * rows - width
    inside = jnp.logical_and(global_row >= 0, global_row < rows * lax.axis_size("lat"))
    wet_x = wet_x * inside.astype(jnp.float32)[:, None]

    regridded = regrid(partner, regrid_map[0])
    flux = exchange_rate[0] * sea * (regridded - surface)
    flux_x = halo8(flux, width - 1)

    for step in range(SUB):
        e = width - 1 - step
        q = advance(
            q,
            crop(wet_x, width - 1 - e),
            crop(zonal_x, width - e),
            crop(meridional_x, width - e),
            crop(mixing_x, width - e),
            crop(flux_x, width - 1 - e),
        )
    return (q[None], flux[None])


def solution(mesh):
    return jax.shard_map(
        shards,
        mesh=mesh,
        in_specs=(
            P("sec", None, None, "lat", "lon"),
            P("sec", None, "lat", "lon"),
            P("sec", None, "lat", "lon"),
            P("sec", None, "lat", "lon"),
            P("sec", "lat", "lon"),
            P("sec", "lat", "lon"),
            P("sec", None, "lat", "lon"),
        ),
        out_specs=(P("sec", None, None, "lat", "lon"), P("sec", None, "lat", "lon")),
        check_vma=False,
    )
```

```python
import jax
import jax.numpy as jnp
from jax import lax
from jax.sharding import PartitionSpec as P

TAPS = 4
SUB = 4
ROW_REACH = 2
COL_REACH = 3


def shifted(x, axis, step):
    count = lax.axis_size(axis)
    return lax.ppermute(x, axis, [(i, (i + step) % count) for i in range(count)])


def halo2(x, w):
    top = shifted(x[:, -w:, :], "lat", 1)
    bottom = shifted(x[:, :w, :], "lat", -1)
    x = jnp.concatenate([top, x, bottom], axis=1)
    left = shifted(x[:, :, -w:], "lon", 1)
    right = shifted(x[:, :, :w], "lon", -1)
    return jnp.concatenate([left, x, right], axis=2)


def regrid(partner, table):
    fields, rows, cols = partner.shape
    row = lax.broadcasted_iota(jnp.int32, (rows, cols), 0)
    col = lax.broadcasted_iota(jnp.int32, (rows, cols), 1)
    d_row = table // cols - row
    d_col = table % cols - col
    d_col = jnp.where(d_col > cols // 2, d_col - cols, d_col)
    d_col = jnp.where(d_col < -(cols // 2), d_col + cols, d_col)
    padded = jnp.concatenate(
        [jnp.repeat(partner[:, :1], ROW_REACH, axis=1), partner, jnp.repeat(partner[:, -1:], ROW_REACH, axis=1)],
        axis=1,
    )
    moved = {}
    for a in range(-ROW_REACH, ROW_REACH + 1):
        rows_a = padded[:, ROW_REACH + a : ROW_REACH + a + rows]
        for b in range(-COL_REACH, COL_REACH + 1):
            moved[a, b] = jnp.roll(rows_a, -b, axis=2)
    total = None
    for tap in range(TAPS):
        picked = moved[0, 0]
        for (a, b), values in moved.items():
            hit = jnp.logical_and(d_row[tap] == a, d_col[tap] == b)
            picked = jnp.where(hit[None], values, picked)
        total = picked if total is None else total + picked
    return total / TAPS


def advance(q, wet, zonal, meridional, mixing, flux):
    center = q[..., 1:-1, 1:-1]
    west = q[..., 1:-1, :-2]
    east = q[..., 1:-1, 2:]
    south = q[..., :-2, 1:-1]
    north = q[..., 2:, 1:-1]
    wet_c = wet[1:-1, 1:-1]
    wet_w = wet[1:-1, :-2]
    wet_e = wet[1:-1, 2:]
    wet_s = wet[:-2, 1:-1]
    wet_n = wet[2:, 1:-1]
    horiz = (
        (wet_w * jnp.maximum(zonal, 0.0)) * (west - center)
        + (wet_e * jnp.maximum(-zonal, 0.0)) * (east - center)
        + (wet_s * jnp.maximum(meridional, 0.0)) * (south - center)
        + (wet_n * jnp.maximum(-meridional, 0.0)) * (north - center)
    )
    down = mixing[:-1] * (center[:, 1:] - center[:, :-1])
    vert = jnp.pad(down, ((0, 0), (0, 1), (0, 0), (0, 0))) - jnp.pad(
        down, ((0, 0), (1, 0), (0, 0), (0, 0))
    )
    updated = center + wet_c * (horiz + vert)
    return jnp.concatenate([updated[:, :1] + flux[:, None], updated[:, 1:]], axis=1)


def crop(x, e):
    if e == 0:
        return x
    return x[..., e:-e, e:-e]


def shards(state, zonal, meridional, mixing, exchange_rate, sea_mask, regrid_map):
    tracers = state[0]
    fields, levels, rows, cols = tracers.shape
    section = lax.axis_index("sec")
    sea = sea_mask[0].astype(jnp.float32)
    wet = jnp.where(section == 1, sea, jnp.ones_like(sea))
    surface = tracers[:, 0]
    partner = lax.ppermute(surface, "sec", [(0, 1), (1, 0)])

    regridded = regrid(partner, regrid_map[0])
    flux = exchange_rate[0] * sea * (regridded - surface)

    width = SUB
    stack = jnp.concatenate(
        [tracers.reshape(fields * levels, rows, cols), zonal[0], meridional[0], mixing[0], wet[None], flux], axis=0
    )
    ext = halo2(stack, width)
    n_q = fields * levels
    q = ext[:n_q].reshape(fields, levels, rows + 2 * width, cols + 2 * width)
    zonal_x = ext[n_q : n_q + levels]
    meridional_x = ext[n_q + levels : n_q + 2 * levels]
    mixing_x = ext[n_q + 2 * levels : n_q + 3 * levels]
    wet_x = ext[n_q + 3 * levels]
    flux_x = ext[n_q + 3 * levels + 1 :]
    row_block = lax.axis_index("lat")
    global_row = jnp.arange(rows + 2 * width, dtype=jnp.int32) + row_block * rows - width
    inside = jnp.logical_and(global_row >= 0, global_row < rows * lax.axis_size("lat"))
    wet_x = wet_x * inside.astype(jnp.float32)[:, None]

    for step in range(SUB):
        e = width - 1 - step
        q = advance(
            q,
            crop(wet_x, width - 1 - e),
            crop(zonal_x, width - e),
            crop(meridional_x, width - e),
            crop(mixing_x, width - e),
            crop(flux_x, width - e),
        )
    return (q[None], flux[None])


def solution(mesh):
    return jax.shard_map(
        shards,
        mesh=mesh,
        in_specs=(
            P("sec", None, None, "lat", "lon"),
            P("sec", None, "lat", "lon"),
            P("sec", None, "lat", "lon"),
            P("sec", None, "lat", "lon"),
            P("sec", "lat", "lon"),
            P("sec", "lat", "lon"),
            P("sec", None, "lat", "lon"),
        ),
        out_specs=(P("sec", None, None, "lat", "lon"), P("sec", None, "lat", "lon")),
        check_vma=False,
    )
```

```python
import functools

import jax
import jax.numpy as jnp
from jax import lax
from jax.experimental import pallas as pl
from jax.experimental.pallas import tpu as pltpu
from jax.sharding import PartitionSpec as P

TAPS = 4
SUB = 4
ROW_REACH = 2
COL_REACH = 3
LANES = 128
HALF = 64
COL_PAD = 8
INTERPRET = False


def shifted(x, axis, step):
    count = lax.axis_size(axis)
    return lax.ppermute(x, axis, [(i, (i + step) % count) for i in range(count)])


def regrid(partner, table):
    fields, rows, cols = partner.shape
    row = lax.broadcasted_iota(jnp.int32, (rows, cols), 0)
    col = lax.broadcasted_iota(jnp.int32, (rows, cols), 1)
    d_row = table // cols - row
    d_col = table % cols - col
    d_col = jnp.where(d_col > cols // 2, d_col - cols, d_col)
    d_col = jnp.where(d_col < -(cols // 2), d_col + cols, d_col)
    padded = jnp.concatenate(
        [jnp.repeat(partner[:, :1], ROW_REACH, axis=1), partner, jnp.repeat(partner[:, -1:], ROW_REACH, axis=1)],
        axis=1,
    )
    moved = {}
    for a in range(-ROW_REACH, ROW_REACH + 1):
        rows_a = padded[:, ROW_REACH + a : ROW_REACH + a + rows]
        for b in range(-COL_REACH, COL_REACH + 1):
            moved[a, b] = jnp.roll(rows_a, -b, axis=2)
    total = None
    for tap in range(TAPS):
        picked = moved[0, 0]
        for (a, b), values in moved.items():
            hit = jnp.logical_and(d_row[tap] == a, d_col[tap] == b)
            picked = jnp.where(hit[None], values, picked)
        total = picked if total is None else total + picked
    return total / TAPS


def steps_kernel(x_ref, top_ref, bot_ref, left_ref, right_ref, o_ref,
                 s_ref, qa_ref, qb_ref, cw_ref, ce_ref, cs_ref, cn_ref, wc_ref, mx_ref, fl_ref, *, levels, width):
    rows, cols = x_ref.shape[0], x_ref.shape[1]
    ext_rows = rows + 2 * width
    ext_cols = cols + 2 * COL_PAD
    s_ref[width : width + rows, COL_PAD : COL_PAD + cols, :] = x_ref[...]
    s_ref[0:width, COL_PAD : COL_PAD + cols, :] = top_ref[...]
    s_ref[width + rows :, COL_PAD : COL_PAD + cols, :] = bot_ref[...]
    s_ref[:, 0:COL_PAD, :] = left_ref[...]
    s_ref[:, COL_PAD + cols :, :] = right_ref[...]

    lane = lax.broadcasted_iota(jnp.int32, (ext_cols, LANES), 1)
    low = lane < HALF
    level = lane % HALF
    down_ok = level < levels - 1
    level0 = level == 0

    def swap_halves(v):
        return pltpu.roll(v, HALF, 1)

    def wet_of(v):
        return jnp.where(low, swap_halves(v), v)

    def coef_row(r, carry):
        v1 = s_ref[r, :, LANES : 2 * LANES]
        v2 = s_ref[r, :, 2 * LANES : 3 * LANES]
        zon = jnp.where(low, v1, swap_halves(v1))
        mer = jnp.where(low, swap_halves(v1), v1)
        mix = jnp.where(low, v2, swap_halves(v2))
        wet_c = wet_of(v2)
        wet_s = wet_of(s_ref[r - 1, :, 2 * LANES : 3 * LANES])
        wet_n = wet_of(s_ref[r + 1, :, 2 * LANES : 3 * LANES])
        wet_w = pltpu.roll(wet_c, 1, 0)
        wet_e = pltpu.roll(wet_c, ext_cols - 1, 0)
        cw_ref[r] = wet_w * jnp.maximum(zon, 0.0)
        ce_ref[r] = wet_e * jnp.maximum(-zon, 0.0)
        cs_ref[r] = wet_s * jnp.maximum(mer, 0.0)
        cn_ref[r] = wet_n * jnp.maximum(-mer, 0.0)
        wc_ref[r] = wet_c
        mx_ref[r] = mix
        fl_ref[r] = pltpu.roll(s_ref[r, :, 0:LANES], LANES - levels, 1)
        return carry

    lax.fori_loop(1, ext_rows - 1, coef_row, 0)
    qa_ref[...] = s_ref[:, :, 0:LANES]

    def step(src, dst):
        def body(r, carry):
            qc = src[r]
            qs = src[r - 1]
            qn = src[r + 1]
            qw = pltpu.roll(qc, 1, 0)
            qe = pltpu.roll(qc, ext_cols - 1, 0)
            horiz = (
                cw_ref[r] * (qw - qc)
                + ce_ref[r] * (qe - qc)
                + cs_ref[r] * (qs - qc)
                + cn_ref[r] * (qn - qc)
            )
            up = pltpu.roll(qc, LANES - 1, 1)
            down = jnp.where(down_ok, mx_ref[r] * (up - qc), 0.0)
            vert = down - pltpu.roll(down, 1, 1)
            updated = qc + wc_ref[r] * (horiz + vert)
            dst[r] = jnp.where(level0, updated + fl_ref[r], updated)
            return carry

        lax.fori_loop(1, ext_rows - 1, body, 0)

    for k in range(SUB):
        if k % 2 == 0:
            step(qa_ref, qb_ref)
        else:
            step(qb_ref, qa_ref)
    final = qa_ref if SUB % 2 == 0 else qb_ref
    o_ref[...] = final[width : width + rows, COL_PAD : COL_PAD + cols, :]


def run_steps(x, top, bot, left, right, levels, width):
    rows, cols, _ = x.shape
    ext = (rows + 2 * width, cols + 2 * COL_PAD, LANES)
    scratch = [pltpu.VMEM((rows + 2 * width, cols + 2 * COL_PAD, 3 * LANES), jnp.float32)]
    scratch += [pltpu.VMEM(ext, jnp.float32) for _ in range(9)]
    return pl.pallas_call(
        functools.partial(steps_kernel, levels=levels, width=width),
        out_shape=jax.ShapeDtypeStruct((rows, cols, LANES), jnp.float32),
        scratch_shapes=scratch,
        compiler_params=pltpu.CompilerParams(vmem_limit_bytes=60 * 1024 * 1024),
        interpret=INTERPRET,
    )(x, top, bot, left, right)


def to_lanes(x, fill):
    return jnp.concatenate([jnp.transpose(x, (1, 2, 0)), fill], axis=-1)


def shards(state, zonal, meridional, mixing, exchange_rate, sea_mask, regrid_map):
    tracers = state[0]
    fields, levels, rows, cols = tracers.shape
    section = lax.axis_index("sec")
    sea = sea_mask[0].astype(jnp.float32)
    wet = jnp.where(section == 1, sea, jnp.ones_like(sea))
    surface = tracers[:, 0]
    partner = lax.ppermute(surface, "sec", [(0, 1), (1, 0)])

    regridded = regrid(partner, regrid_map[0])
    flux = exchange_rate[0] * sea * (regridded - surface)

    pad = HALF - levels
    zeros = jnp.zeros((rows, cols, pad), jnp.float32)
    flux_pad = [jnp.concatenate([flux[f][:, :, None], zeros[:, :, 1:]], axis=-1) for f in range(fields)]
    x = jnp.concatenate(
        [to_lanes(tracers[0], flux_pad[0]), to_lanes(tracers[1], flux_pad[1]),
         to_lanes(zonal[0], zeros), to_lanes(meridional[0], zeros),
         to_lanes(mixing[0], zeros), jnp.broadcast_to(wet[:, :, None], (rows, cols, HALF))],
        axis=-1,
    )

    width = SUB
    top = shifted(x[-width:], "lat", 1)
    bot = shifted(x[:width], "lat", -1)
    row_block = lax.axis_index("lat")
    wet_lane = lax.broadcasted_iota(jnp.int32, (1, 1, 3 * LANES), 2) >= 2 * LANES + HALF
    top = jnp.where(jnp.logical_and(wet_lane, row_block == 0), 0.0, top)
    bot = jnp.where(jnp.logical_and(wet_lane, row_block == lax.axis_size("lat") - 1), 0.0, bot)
    left = shifted(jnp.concatenate([top[:, -COL_PAD:], x[:, -COL_PAD:], bot[:, -COL_PAD:]], axis=0), "lon", 1)
    right = shifted(jnp.concatenate([top[:, :COL_PAD], x[:, :COL_PAD], bot[:, :COL_PAD]], axis=0), "lon", -1)

    out = run_steps(x, top, bot, left, right, levels, width)
    q = out.reshape(rows, cols, fields, HALF)[..., :levels]
    q = jnp.transpose(q, (2, 3, 0, 1))
    return (q[None], flux[None])


def solution(mesh):
    return jax.shard_map(
        shards,
        mesh=mesh,
        in_specs=(
            P("sec", None, None, "lat", "lon"),
            P("sec", None, "lat", "lon"),
            P("sec", None, "lat", "lon"),
            P("sec", None, "lat", "lon"),
            P("sec", "lat", "lon"),
            P("sec", "lat", "lon"),
            P("sec", None, "lat", "lon"),
        ),
        out_specs=(P("sec", None, None, "lat", "lon"), P("sec", None, "lat", "lon")),
        check_vma=False,
    )
```

```python
import functools

import jax
import jax.numpy as jnp
from jax import lax
from jax.experimental import pallas as pl
from jax.experimental.pallas import tpu as pltpu
from jax.sharding import PartitionSpec as P

TAPS = 4
SUB = 4
ROW_REACH = 2
COL_REACH = 3
LANES = 128
HALF = 64
COL_PAD = 8
INTERPRET = False


def shifted(x, axis, step):
    count = lax.axis_size(axis)
    return lax.ppermute(x, axis, [(i, (i + step) % count) for i in range(count)])


def regrid(partner, table):
    fields, rows, cols = partner.shape
    row = lax.broadcasted_iota(jnp.int32, (rows, cols), 0)
    col = lax.broadcasted_iota(jnp.int32, (rows, cols), 1)
    d_row = table // cols - row
    d_col = table % cols - col
    d_col = jnp.where(d_col > cols // 2, d_col - cols, d_col)
    d_col = jnp.where(d_col < -(cols // 2), d_col + cols, d_col)
    padded = jnp.concatenate(
        [jnp.repeat(partner[:, :1], ROW_REACH, axis=1), partner, jnp.repeat(partner[:, -1:], ROW_REACH, axis=1)],
        axis=1,
    )
    moved = {}
    for a in range(-ROW_REACH, ROW_REACH + 1):
        rows_a = padded[:, ROW_REACH + a : ROW_REACH + a + rows]
        for b in range(-COL_REACH, COL_REACH + 1):
            moved[a, b] = jnp.roll(rows_a, -b, axis=2)
    total = None
    for tap in range(TAPS):
        picked = moved[0, 0]
        for (a, b), values in moved.items():
            hit = jnp.logical_and(d_row[tap] == a, d_col[tap] == b)
            picked = jnp.where(hit[None], values, picked)
        total = picked if total is None else total + picked
    return total / TAPS


def steps_kernel(xq_ref, topq_ref, botq_ref, leftq_ref, rightq_ref, xv_ref, topv_ref, botv_ref, leftv_ref, rightv_ref,
                 o_ref, s_ref, qa_ref, qb_ref, cw_ref, ce_ref, cs_ref, cn_ref, wc_ref, mx_ref, fl_ref, *, levels, width):
    rows, cols = xq_ref.shape[0], xq_ref.shape[1]
    ext_rows = rows + 2 * width
    ext_cols = cols + 2 * COL_PAD
    for lo, hi, x_ref, top_ref, bot_ref, left_ref, right_ref in (
        (0, LANES, xq_ref, topq_ref, botq_ref, leftq_ref, rightq_ref),
        (LANES, 3 * LANES, xv_ref, topv_ref, botv_ref, leftv_ref, rightv_ref),
    ):
        s_ref[width : width + rows, COL_PAD : COL_PAD + cols, lo:hi] = x_ref[...]
        s_ref[0:width, COL_PAD : COL_PAD + cols, lo:hi] = top_ref[...]
        s_ref[width + rows :, COL_PAD : COL_PAD + cols, lo:hi] = bot_ref[...]
        s_ref[:, 0:COL_PAD, lo:hi] = left_ref[...]
        s_ref[:, COL_PAD + cols :, lo:hi] = right_ref[...]

    lane = lax.broadcasted_iota(jnp.int32, (ext_cols, LANES), 1)
    low = lane < HALF
    level = lane % HALF
    down_ok = level < levels - 1
    level0 = level == 0

    def swap_halves(v):
        return pltpu.roll(v, HALF, 1)

    def wet_of(v):
        return jnp.where(low, swap_halves(v), v)

    def coef_row(r, carry):
        v1 = s_ref[r, :, LANES : 2 * LANES]
        v2 = s_ref[r, :, 2 * LANES : 3 * LANES]
        zon = jnp.where(low, v1, swap_halves(v1))
        mer = jnp.where(low, swap_halves(v1), v1)
        mix = jnp.where(low, v2, swap_halves(v2))
        wet_c = wet_of(v2)
        wet_s = wet_of(s_ref[r - 1, :, 2 * LANES : 3 * LANES])
        wet_n = wet_of(s_ref[r + 1, :, 2 * LANES : 3 * LANES])
        wet_w = pltpu.roll(wet_c, 1, 0)
        wet_e = pltpu.roll(wet_c, ext_cols - 1, 0)
        cw_ref[r] = wet_w * jnp.maximum(zon, 0.0)
        ce_ref[r] = wet_e * jnp.maximum(-zon, 0.0)
        cs_ref[r] = wet_s * jnp.maximum(mer, 0.0)
        cn_ref[r] = wet_n * jnp.maximum(-mer, 0.0)
        wc_ref[r] = wet_c
        mx_ref[r] = mix
        fl_ref[r] = pltpu.roll(s_ref[r, :, 0:LANES], LANES - levels, 1)
        return carry

    lax.fori_loop(1, ext_rows - 1, coef_row, 0)
    qa_ref[...] = s_ref[:, :, 0:LANES]

    def step(src, dst, k):
        def body(r, carry):
            qc = src[r]
            qs = src[r - 1]
            qn = src[r + 1]
            qw = pltpu.roll(qc, 1, 0)
            qe = pltpu.roll(qc, ext_cols - 1, 0)
            horiz = (
                cw_ref[r] * (qw - qc)
                + ce_ref[r] * (qe - qc)
                + cs_ref[r] * (qs - qc)
                + cn_ref[r] * (qn - qc)
            )
            up = pltpu.roll(qc, LANES - 1, 1)
            down = jnp.where(down_ok, mx_ref[r] * (up - qc), 0.0)
            vert = down - pltpu.roll(down, 1, 1)
            updated = qc + wc_ref[r] * (horiz + vert)
            dst[r] = jnp.where(level0, updated + fl_ref[r], updated)
            return carry

        lax.fori_loop(k + 1, ext_rows - 1 - k, body, 0)

    for k in range(SUB):
        if k % 2 == 0:
            step(qa_ref, qb_ref, k)
        else:
            step(qb_ref, qa_ref, k)
    final = qa_ref if SUB % 2 == 0 else qb_ref
    o_ref[...] = final[width : width + rows, COL_PAD : COL_PAD + cols, :]


def run_steps(q_parts, v_parts, levels, width):
    rows, cols, _ = q_parts[0].shape
    ext = (rows + 2 * width, cols + 2 * COL_PAD, LANES)
    scratch = [pltpu.VMEM((rows + 2 * width, cols + 2 * COL_PAD, 3 * LANES), jnp.float32)]
    scratch += [pltpu.VMEM(ext, jnp.float32) for _ in range(9)]
    return pl.pallas_call(
        functools.partial(steps_kernel, levels=levels, width=width),
        out_shape=jax.ShapeDtypeStruct((rows, cols, LANES), jnp.float32),
        scratch_shapes=scratch,
        compiler_params=pltpu.CompilerParams(vmem_limit_bytes=60 * 1024 * 1024),
        interpret=INTERPRET,
    )(*q_parts, *v_parts)


def lanes_last(planes):
    return jnp.transpose(jnp.concatenate(planes, axis=0), (1, 2, 0))


def halo_parts(x, width, mask=None):
    top = shifted(x[-width:], "lat", 1)
    bot = shifted(x[:width], "lat", -1)
    if mask is not None:
        row_block = lax.axis_index("lat")
        top = jnp.where(jnp.logical_and(mask, row_block == 0), 0.0, top)
        bot = jnp.where(jnp.logical_and(mask, row_block == lax.axis_size("lat") - 1), 0.0, bot)
    left = shifted(jnp.concatenate([top[:, -COL_PAD:], x[:, -COL_PAD:], bot[:, -COL_PAD:]], axis=0), "lon", 1)
    right = shifted(jnp.concatenate([top[:, :COL_PAD], x[:, :COL_PAD], bot[:, :COL_PAD]], axis=0), "lon", -1)
    return (x, top, bot, left, right)


def shards(state, zonal, meridional, mixing, exchange_rate, sea_mask, regrid_map):
    tracers = state[0]
    fields, levels, rows, cols = tracers.shape
    section = lax.axis_index("sec")
    sea = sea_mask[0].astype(jnp.float32)
    wet = jnp.where(section == 1, sea, jnp.ones_like(sea))
    width = SUB
    gap = jnp.zeros((HALF - levels, rows, cols), jnp.float32)

    xv = lanes_last([zonal[0], gap, meridional[0], gap, mixing[0], gap, jnp.broadcast_to(wet, (HALF, rows, cols))])
    wet_lane = lax.broadcasted_iota(jnp.int32, (1, 1, 2 * LANES), 2) >= LANES + HALF
    v_parts = halo_parts(xv, width, wet_lane)

    surface = tracers[:, 0]
    partner = lax.ppermute(surface, "sec", [(0, 1), (1, 0)])
    regridded = regrid(partner, regrid_map[0])
    flux = exchange_rate[0] * sea * (regridded - surface)

    planes = []
    for f in range(fields):
        planes += [tracers[f], flux[f][None], gap[1:]]
    xq = lanes_last(planes)
    q_parts = halo_parts(xq, width)

    out = run_steps(q_parts, v_parts, levels, width)
    q = jnp.transpose(out, (2, 0, 1)).reshape(fields, HALF, rows, cols)[:, :levels]
    return (q[None], flux[None])


def solution(mesh):
    return jax.shard_map(
        shards,
        mesh=mesh,
        in_specs=(
            P("sec", None, None, "lat", "lon"),
            P("sec", None, "lat", "lon"),
            P("sec", None, "lat", "lon"),
            P("sec", None, "lat", "lon"),
            P("sec", "lat", "lon"),
            P("sec", "lat", "lon"),
            P("sec", None, "lat", "lon"),
        ),
        out_specs=(P("sec", None, None, "lat", "lon"), P("sec", None, "lat", "lon")),
        check_vma=False,
    )
```

```python
import functools

import jax
import jax.numpy as jnp
from jax import lax
from jax.experimental import pallas as pl
from jax.experimental.pallas import tpu as pltpu
from jax.sharding import PartitionSpec as P

TAPS = 4
SUB = 4
ROW_REACH = 2
COL_REACH = 3
LANES = 128
HALF = 64
COL_PAD = 8
INTERPRET = False


def shifted(x, axis, step):
    count = lax.axis_size(axis)
    return lax.ppermute(x, axis, [(i, (i + step) % count) for i in range(count)])


def shifted2(x, da, db):
    n_lat = lax.axis_size("lat")
    n_lon = lax.axis_size("lon")
    pairs = [
        (a * n_lon + b, ((a + da) % n_lat) * n_lon + (b + db) % n_lon) for a in range(n_lat) for b in range(n_lon)
    ]
    return lax.ppermute(x, ("lat", "lon"), pairs)


def regrid(partner, table):
    fields, rows, cols = partner.shape
    row = lax.broadcasted_iota(jnp.int32, (rows, cols), 0)
    col = lax.broadcasted_iota(jnp.int32, (rows, cols), 1)
    d_row = table // cols - row
    d_col = table % cols - col
    d_col = jnp.where(d_col > cols // 2, d_col - cols, d_col)
    d_col = jnp.where(d_col < -(cols // 2), d_col + cols, d_col)
    padded = jnp.concatenate(
        [jnp.repeat(partner[:, :1], ROW_REACH, axis=1), partner, jnp.repeat(partner[:, -1:], ROW_REACH, axis=1)],
        axis=1,
    )
    moved = {}
    for a in range(-ROW_REACH, ROW_REACH + 1):
        rows_a = padded[:, ROW_REACH + a : ROW_REACH + a + rows]
        for b in range(-COL_REACH, COL_REACH + 1):
            moved[a, b] = jnp.roll(rows_a, -b, axis=2)
    total = None
    for tap in range(TAPS):
        picked = moved[0, 0]
        for (a, b), values in moved.items():
            hit = jnp.logical_and(d_row[tap] == a, d_col[tap] == b)
            picked = jnp.where(hit[None], values, picked)
        total = picked if total is None else total + picked
    return total / TAPS


def steps_kernel(x_ref, top_ref, bot_ref, left_ref, right_ref, o_ref,
                 s_ref, qa_ref, qb_ref, cw_ref, ce_ref, cs_ref, cn_ref, wc_ref, mx_ref, fl_ref, *, levels, width):
    rows, cols = x_ref.shape[0], x_ref.shape[1]
    ext_rows = rows + 2 * width
    ext_cols = cols + 2 * COL_PAD
    s_ref[width : width + rows, COL_PAD : COL_PAD + cols, :] = x_ref[...]
    s_ref[0:width, COL_PAD : COL_PAD + cols, :] = top_ref[...]
    s_ref[width + rows :, COL_PAD : COL_PAD + cols, :] = bot_ref[...]
    s_ref[:, 0:COL_PAD, :] = left_ref[...]
    s_ref[:, COL_PAD + cols :, :] = right_ref[...]

    lane = lax.broadcasted_iota(jnp.int32, (ext_cols, LANES), 1)
    low = lane < HALF
    level = lane % HALF
    down_ok = level < levels - 1
    level0 = level == 0

    def swap_halves(v):
        return pltpu.roll(v, HALF, 1)

    def wet_of(v):
        return jnp.where(low, swap_halves(v), v)

    def coef_row(r, carry):
        v1 = s_ref[r, :, LANES : 2 * LANES]
        v2 = s_ref[r, :, 2 * LANES : 3 * LANES]
        zon = jnp.where(low, v1, swap_halves(v1))
        mer = jnp.where(low, swap_halves(v1), v1)
        mix = jnp.where(low, v2, swap_halves(v2))
        wet_c = wet_of(v2)
        wet_s = wet_of(s_ref[r - 1, :, 2 * LANES : 3 * LANES])
        wet_n = wet_of(s_ref[r + 1, :, 2 * LANES : 3 * LANES])
        wet_w = pltpu.roll(wet_c, 1, 0)
        wet_e = pltpu.roll(wet_c, ext_cols - 1, 0)
        cw_ref[r] = wet_w * jnp.maximum(zon, 0.0)
        ce_ref[r] = wet_e * jnp.maximum(-zon, 0.0)
        cs_ref[r] = wet_s * jnp.maximum(mer, 0.0)
        cn_ref[r] = wet_n * jnp.maximum(-mer, 0.0)
        wc_ref[r] = wet_c
        mx_ref[r] = mix
        fl_ref[r] = pltpu.roll(s_ref[r, :, 0:LANES], LANES - levels, 1)
        return carry

    lax.fori_loop(1, ext_rows - 1, coef_row, 0)
    qa_ref[...] = s_ref[:, :, 0:LANES]

    def step(src, dst):
        def body(r, carry):
            qc = src[r]
            qs = src[r - 1]
            qn = src[r + 1]
            qw = pltpu.roll(qc, 1, 0)
            qe = pltpu.roll(qc, ext_cols - 1, 0)
            horiz = (
                cw_ref[r] * (qw - qc)
                + ce_ref[r] * (qe - qc)
                + cs_ref[r] * (qs - qc)
                + cn_ref[r] * (qn - qc)
            )
            up = pltpu.roll(qc, LANES - 1, 1)
            down = jnp.where(down_ok, mx_ref[r] * (up - qc), 0.0)
            vert = down - pltpu.roll(down, 1, 1)
            updated = qc + wc_ref[r] * (horiz + vert)
            dst[r] = jnp.where(level0, updated + fl_ref[r], updated)
            return carry

        lax.fori_loop(1, ext_rows - 1, body, 0)

    for k in range(SUB):
        if k % 2 == 0:
            step(qa_ref, qb_ref)
        else:
            step(qb_ref, qa_ref)
    final = qa_ref if SUB % 2 == 0 else qb_ref
    o_ref[...] = final[width : width + rows, COL_PAD : COL_PAD + cols, :]


def run_steps(x, top, bot, left, right, levels, width):
    rows, cols, _ = x.shape
    ext = (rows + 2 * width, cols + 2 * COL_PAD, LANES)
    scratch = [pltpu.VMEM((rows + 2 * width, cols + 2 * COL_PAD, 3 * LANES), jnp.float32)]
    scratch += [pltpu.VMEM(ext, jnp.float32) for _ in range(9)]
    return pl.pallas_call(
        functools.partial(steps_kernel, levels=levels, width=width),
        out_shape=jax.ShapeDtypeStruct((rows, cols, LANES), jnp.float32),
        scratch_shapes=scratch,
        compiler_params=pltpu.CompilerParams(vmem_limit_bytes=60 * 1024 * 1024),
        interpret=INTERPRET,
    )(x, top, bot, left, right)


def to_lanes(x, fill):
    return jnp.concatenate([jnp.transpose(x, (1, 2, 0)), fill], axis=-1)


def shards(state, zonal, meridional, mixing, exchange_rate, sea_mask, regrid_map):
    tracers = state[0]
    fields, levels, rows, cols = tracers.shape
    section = lax.axis_index("sec")
    sea = sea_mask[0].astype(jnp.float32)
    wet = jnp.where(section == 1, sea, jnp.ones_like(sea))
    surface = tracers[:, 0]
    partner = lax.ppermute(surface, "sec", [(0, 1), (1, 0)])

    regridded = regrid(partner, regrid_map[0])
    flux = exchange_rate[0] * sea * (regridded - surface)

    pad = HALF - levels
    zeros = jnp.zeros((rows, cols, pad), jnp.float32)
    flux_pad = [jnp.concatenate([flux[f][:, :, None], zeros[:, :, 1:]], axis=-1) for f in range(fields)]
    x = jnp.concatenate(
        [to_lanes(tracers[0], flux_pad[0]), to_lanes(tracers[1], flux_pad[1]),
         to_lanes(zonal[0], zeros), to_lanes(meridional[0], zeros),
         to_lanes(mixing[0], zeros), jnp.broadcast_to(wet[:, :, None], (rows, cols, HALF))],
        axis=-1,
    )

    width = SUB
    row_block = lax.axis_index("lat")
    wet_lane = lax.broadcasted_iota(jnp.int32, (1, 1, 3 * LANES), 2) >= 2 * LANES + HALF
    top_mask = jnp.logical_and(wet_lane, row_block == 0)
    bot_mask = jnp.logical_and(wet_lane, row_block == lax.axis_size("lat") - 1)
    top = jnp.where(top_mask, 0.0, shifted2(x[-width:], 1, 0))
    bot = jnp.where(bot_mask, 0.0, shifted2(x[:width], -1, 0))
    mid_left = shifted2(x[:, -COL_PAD:], 0, 1)
    mid_right = shifted2(x[:, :COL_PAD], 0, -1)
    top_left = jnp.where(top_mask, 0.0, shifted2(x[-width:, -COL_PAD:], 1, 1))
    top_right = jnp.where(top_mask, 0.0, shifted2(x[-width:, :COL_PAD], 1, -1))
    bot_left = jnp.where(bot_mask, 0.0, shifted2(x[:width, -COL_PAD:], -1, 1))
    bot_right = jnp.where(bot_mask, 0.0, shifted2(x[:width, :COL_PAD], -1, -1))
    left = jnp.concatenate([top_left, mid_left, bot_left], axis=0)
    right = jnp.concatenate([top_right, mid_right, bot_right], axis=0)

    out = run_steps(x, top, bot, left, right, levels, width)
    q = out.reshape(rows, cols, fields, HALF)[..., :levels]
    q = jnp.transpose(q, (2, 3, 0, 1))
    return (q[None], flux[None])


def solution(mesh):
    return jax.shard_map(
        shards,
        mesh=mesh,
        in_specs=(
            P("sec", None, None, "lat", "lon"),
            P("sec", None, "lat", "lon"),
            P("sec", None, "lat", "lon"),
            P("sec", None, "lat", "lon"),
            P("sec", "lat", "lon"),
            P("sec", "lat", "lon"),
            P("sec", None, "lat", "lon"),
        ),
        out_specs=(P("sec", None, None, "lat", "lon"), P("sec", None, "lat", "lon")),
        check_vma=False,
    )
```

```python
import functools

import jax
import jax.numpy as jnp
from jax import lax
from jax.experimental import pallas as pl
from jax.experimental.pallas import tpu as pltpu
from jax.sharding import PartitionSpec as P

TAPS = 4
SUB = 4
ROW_REACH = 2
COL_REACH = 3
LANES = 128
HALF = 64
COL_PAD = 8
INTERPRET = False


def shifted(x, axis, step):
    count = lax.axis_size(axis)
    return lax.ppermute(x, axis, [(i, (i + step) % count) for i in range(count)])


def regrid(partner, table):
    fields, rows, cols = partner.shape
    row = lax.broadcasted_iota(jnp.int32, (rows, cols), 0)
    col = lax.broadcasted_iota(jnp.int32, (rows, cols), 1)
    d_row = table // cols - row
    d_col = table % cols - col
    d_col = jnp.where(d_col > cols // 2, d_col - cols, d_col)
    d_col = jnp.where(d_col < -(cols // 2), d_col + cols, d_col)
    padded = jnp.concatenate(
        [jnp.repeat(partner[:, :1], ROW_REACH, axis=1), partner, jnp.repeat(partner[:, -1:], ROW_REACH, axis=1)],
        axis=1,
    )
    moved = {}
    for a in range(-ROW_REACH, ROW_REACH + 1):
        rows_a = padded[:, ROW_REACH + a : ROW_REACH + a + rows]
        for b in range(-COL_REACH, COL_REACH + 1):
            moved[a, b] = jnp.roll(rows_a, -b, axis=2)
    total = None
    for tap in range(TAPS):
        picked = moved[0, 0]
        for (a, b), values in moved.items():
            hit = jnp.logical_and(d_row[tap] == a, d_col[tap] == b)
            picked = jnp.where(hit[None], values, picked)
        total = picked if total is None else total + picked
    return total / TAPS


def steps_kernel(x_ref, top_ref, bot_ref, left_ref, right_ref, o_ref,
                 s_ref, qa_ref, qb_ref, cw_ref, ce_ref, cs_ref, cn_ref, wc_ref, mx_ref, fl_ref, *, levels, width):
    rows, cols = x_ref.shape[0], x_ref.shape[1]
    ext_rows = rows + 2 * width
    ext_cols = cols + 2 * COL_PAD
    s_ref[width : width + rows, COL_PAD : COL_PAD + cols, :] = x_ref[...]
    s_ref[0:width, COL_PAD : COL_PAD + cols, :] = top_ref[...]
    s_ref[width + rows :, COL_PAD : COL_PAD + cols, :] = bot_ref[...]
    s_ref[:, 0:COL_PAD, :] = left_ref[...]
    s_ref[:, COL_PAD + cols :, :] = right_ref[...]

    lane = lax.broadcasted_iota(jnp.int32, (ext_cols, LANES), 1)
    low = lane < HALF
    level = lane % HALF
    down_ok = level < levels - 1
    level0 = level == 0

    def swap_halves(v):
        return pltpu.roll(v, HALF, 1)

    def wet_of(v):
        return jnp.where(low, swap_halves(v), v)

    def coef_row(r, carry):
        v1 = s_ref[r, :, LANES : 2 * LANES]
        v2 = s_ref[r, :, 2 * LANES : 3 * LANES]
        zon = jnp.where(low, v1, swap_halves(v1))
        mer = jnp.where(low, swap_halves(v1), v1)
        mix = jnp.where(low, v2, swap_halves(v2))
        wet_c = wet_of(v2)
        wet_s = wet_of(s_ref[r - 1, :, 2 * LANES : 3 * LANES])
        wet_n = wet_of(s_ref[r + 1, :, 2 * LANES : 3 * LANES])
        wet_w = pltpu.roll(wet_c, 1, 0)
        wet_e = pltpu.roll(wet_c, ext_cols - 1, 0)
        cw_ref[r] = wet_w * jnp.maximum(zon, 0.0)
        ce_ref[r] = wet_e * jnp.maximum(-zon, 0.0)
        cs_ref[r] = wet_s * jnp.maximum(mer, 0.0)
        cn_ref[r] = wet_n * jnp.maximum(-mer, 0.0)
        wc_ref[r] = wet_c
        mx_ref[r] = mix
        fl_ref[r] = pltpu.roll(s_ref[r, :, 0:LANES], LANES - levels, 1)
        return carry

    lax.fori_loop(1, ext_rows - 1, coef_row, 0)
    qa_ref[...] = s_ref[:, :, 0:LANES]

    def step(src, dst):
        def body(r, carry):
            qc = src[r]
            qs = src[r - 1]
            qn = src[r + 1]
            qw = pltpu.roll(qc, 1, 0)
            qe = pltpu.roll(qc, ext_cols - 1, 0)
            horiz = (
                cw_ref[r] * (qw - qc)
                + ce_ref[r] * (qe - qc)
                + cs_ref[r] * (qs - qc)
                + cn_ref[r] * (qn - qc)
            )
            up = pltpu.roll(qc, LANES - 1, 1)
            down = jnp.where(down_ok, mx_ref[r] * (up - qc), 0.0)
            vert = down - pltpu.roll(down, 1, 1)
            updated = qc + wc_ref[r] * (horiz + vert)
            dst[r] = jnp.where(level0, updated + fl_ref[r], updated)
            return carry

        lax.fori_loop(1, ext_rows - 1, body, 0)

    for k in range(SUB):
        if k % 2 == 0:
            step(qa_ref, qb_ref)
        else:
            step(qb_ref, qa_ref)
    final = qa_ref if SUB % 2 == 0 else qb_ref
    o_ref[...] = final[width : width + rows, COL_PAD : COL_PAD + cols, :]


def run_steps(x, top, bot, left, right, levels, width):
    rows, cols, _ = x.shape
    ext = (rows + 2 * width, cols + 2 * COL_PAD, LANES)
    scratch = [pltpu.VMEM((rows + 2 * width, cols + 2 * COL_PAD, 3 * LANES), jnp.float32)]
    scratch += [pltpu.VMEM(ext, jnp.float32) for _ in range(9)]
    return pl.pallas_call(
        functools.partial(steps_kernel, levels=levels, width=width),
        out_shape=jax.ShapeDtypeStruct((rows, cols, LANES), jnp.float32),
        scratch_shapes=scratch,
        compiler_params=pltpu.CompilerParams(vmem_limit_bytes=60 * 1024 * 1024),
        interpret=INTERPRET,
    )(x, top, bot, left, right)


def pack_kernel(st_ref, zon_ref, mer_ref, mix_ref, wet_ref, flux_ref, o_ref, t0_ref, t1_ref, t2_ref, *, levels):
    rows = wet_ref.shape[0]
    for t_ref in (t0_ref, t1_ref, t2_ref):
        t_ref[...] = jnp.zeros(t_ref.shape, jnp.float32)
    sub = lax.broadcasted_iota(jnp.int32, (LANES, LANES), 0)

    def body(r, carry):
        levels_at = pl.ds(r, levels, stride=rows)
        t0_ref[0:levels] = st_ref[0, levels_at, :]
        t0_ref[HALF : HALF + levels] = st_ref[1, levels_at, :]
        t1_ref[0:levels] = zon_ref[levels_at, :]
        t1_ref[HALF : HALF + levels] = mer_ref[levels_at, :]
        t2_ref[0:levels] = mix_ref[levels_at, :]
        t2_ref[HALF:LANES] = jnp.broadcast_to(wet_ref[pl.ds(r, 1), :], (LANES - HALF, LANES))
        f0 = jnp.broadcast_to(flux_ref[0, pl.ds(r, 1), :], (LANES, LANES))
        f1 = jnp.broadcast_to(flux_ref[1, pl.ds(r, 1), :], (LANES, LANES))
        t0 = t0_ref[...]
        t0 = jnp.where(sub == levels, f0, t0)
        t0 = jnp.where(sub == HALF + levels, f1, t0)
        o_ref[r, :, 0:LANES] = jnp.transpose(t0)
        o_ref[r, :, LANES : 2 * LANES] = jnp.transpose(t1_ref[...])
        o_ref[r, :, 2 * LANES : 3 * LANES] = jnp.transpose(t2_ref[...])
        return carry

    for r in range(rows):
        body(r, 0)


def pack(tracers, zonal, meridional, mixing, wet, flux):
    fields, levels, rows, cols = tracers.shape
    return pl.pallas_call(
        functools.partial(pack_kernel, levels=levels),
        out_shape=jax.ShapeDtypeStruct((rows, cols, 3 * LANES), jnp.float32),
        scratch_shapes=[pltpu.VMEM((LANES, LANES), jnp.float32) for _ in range(3)],
        interpret=INTERPRET,
    )(
        tracers.reshape(fields, levels * rows, cols),
        zonal.reshape(levels * rows, cols),
        meridional.reshape(levels * rows, cols),
        mixing.reshape(levels * rows, cols),
        wet,
        flux,
    )


def to_lanes(x, fill):
    return jnp.concatenate([jnp.transpose(x, (1, 2, 0)), fill], axis=-1)


def shards(state, zonal, meridional, mixing, exchange_rate, sea_mask, regrid_map):
    tracers = state[0]
    fields, levels, rows, cols = tracers.shape
    section = lax.axis_index("sec")
    sea = sea_mask[0].astype(jnp.float32)
    wet = jnp.where(section == 1, sea, jnp.ones_like(sea))
    surface = tracers[:, 0]
    partner = lax.ppermute(surface, "sec", [(0, 1), (1, 0)])

    regridded = regrid(partner, regrid_map[0])
    flux = exchange_rate[0] * sea * (regridded - surface)

    x = pack(tracers, zonal[0], meridional[0], mixing[0], wet, flux)

    width = SUB
    top = shifted(x[-width:], "lat", 1)
    bot = shifted(x[:width], "lat", -1)
    row_block = lax.axis_index("lat")
    wet_lane = lax.broadcasted_iota(jnp.int32, (1, 1, 3 * LANES), 2) >= 2 * LANES + HALF
    top = jnp.where(jnp.logical_and(wet_lane, row_block == 0), 0.0, top)
    bot = jnp.where(jnp.logical_and(wet_lane, row_block == lax.axis_size("lat") - 1), 0.0, bot)
    left = shifted(jnp.concatenate([top[:, -COL_PAD:], x[:, -COL_PAD:], bot[:, -COL_PAD:]], axis=0), "lon", 1)
    right = shifted(jnp.concatenate([top[:, :COL_PAD], x[:, :COL_PAD], bot[:, :COL_PAD]], axis=0), "lon", -1)

    out = run_steps(x, top, bot, left, right, levels, width)
    q = out.reshape(rows, cols, fields, HALF)[..., :levels]
    q = jnp.transpose(q, (2, 3, 0, 1))
    return (q[None], flux[None])


def solution(mesh):
    return jax.shard_map(
        shards,
        mesh=mesh,
        in_specs=(
            P("sec", None, None, "lat", "lon"),
            P("sec", None, "lat", "lon"),
            P("sec", None, "lat", "lon"),
            P("sec", None, "lat", "lon"),
            P("sec", "lat", "lon"),
            P("sec", "lat", "lon"),
            P("sec", None, "lat", "lon"),
        ),
        out_specs=(P("sec", None, None, "lat", "lon"), P("sec", None, "lat", "lon")),
        check_vma=False,
    )
```

```python
import functools

import jax
import jax.numpy as jnp
from jax import lax
from jax.experimental import pallas as pl
from jax.experimental.pallas import tpu as pltpu
from jax.sharding import PartitionSpec as P

TAPS = 4
SUB = 4
ROW_REACH = 2
COL_REACH = 3
LANES = 128
HALF = 64
COL_PAD = 8
INTERPRET = False


def shifted(x, axis, step, cyclic=True):
    count = lax.axis_size(axis)
    pairs = [(i, (i + step) % count) for i in range(count) if cyclic or 0 <= i + step < count]
    return lax.ppermute(x, axis, pairs)


def regrid(partner, table):
    fields, rows, cols = partner.shape
    row = lax.broadcasted_iota(jnp.int32, (rows, cols), 0)
    col = lax.broadcasted_iota(jnp.int32, (rows, cols), 1)
    d_row = table // cols - row
    d_col = table % cols - col
    d_col = jnp.where(d_col > cols // 2, d_col - cols, d_col)
    d_col = jnp.where(d_col < -(cols // 2), d_col + cols, d_col)
    padded = jnp.concatenate(
        [jnp.repeat(partner[:, :1], ROW_REACH, axis=1), partner, jnp.repeat(partner[:, -1:], ROW_REACH, axis=1)],
        axis=1,
    )
    moved = {}
    for a in range(-ROW_REACH, ROW_REACH + 1):
        rows_a = padded[:, ROW_REACH + a : ROW_REACH + a + rows]
        for b in range(-COL_REACH, COL_REACH + 1):
            moved[a, b] = jnp.roll(rows_a, -b, axis=2)
    total = None
    for tap in range(TAPS):
        picked = moved[0, 0]
        for (a, b), values in moved.items():
            hit = jnp.logical_and(d_row[tap] == a, d_col[tap] == b)
            picked = jnp.where(hit[None], values, picked)
        total = picked if total is None else total + picked
    return total / TAPS


def steps_kernel(x_ref, top_ref, bot_ref, left_ref, right_ref, o_ref,
                 s_ref, qa_ref, qb_ref, cw_ref, ce_ref, cs_ref, cn_ref, wc_ref, mx_ref, fl_ref, *, levels, width):
    rows, cols = x_ref.shape[0], x_ref.shape[1]
    ext_rows = rows + 2 * width
    ext_cols = cols + 2 * COL_PAD
    s_ref[width : width + rows, COL_PAD : COL_PAD + cols, :] = x_ref[...]
    s_ref[0:width, COL_PAD : COL_PAD + cols, :] = top_ref[...]
    s_ref[width + rows :, COL_PAD : COL_PAD + cols, :] = bot_ref[...]
    s_ref[:, 0:COL_PAD, :] = left_ref[...]
    s_ref[:, COL_PAD + cols :, :] = right_ref[...]

    lane = lax.broadcasted_iota(jnp.int32, (ext_cols, LANES), 1)
    low = lane < HALF
    level = lane % HALF
    down_ok = level < levels - 1
    level0 = level == 0

    def swap_halves(v):
        return pltpu.roll(v, HALF, 1)

    def wet_of(v):
        return jnp.where(low, swap_halves(v), v)

    def coef_row(r, carry):
        v1 = s_ref[r, :, LANES : 2 * LANES]
        v2 = s_ref[r, :, 2 * LANES : 3 * LANES]
        zon = jnp.where(low, v1, swap_halves(v1))
        mer = jnp.where(low, swap_halves(v1), v1)
        mix = jnp.where(low, v2, swap_halves(v2))
        wet_c = wet_of(v2)
        wet_s = wet_of(s_ref[r - 1, :, 2 * LANES : 3 * LANES])
        wet_n = wet_of(s_ref[r + 1, :, 2 * LANES : 3 * LANES])
        wet_w = pltpu.roll(wet_c, 1, 0)
        wet_e = pltpu.roll(wet_c, ext_cols - 1, 0)
        cw_ref[r] = wet_w * jnp.maximum(zon, 0.0)
        ce_ref[r] = wet_e * jnp.maximum(-zon, 0.0)
        cs_ref[r] = wet_s * jnp.maximum(mer, 0.0)
        cn_ref[r] = wet_n * jnp.maximum(-mer, 0.0)
        wc_ref[r] = wet_c
        mx_ref[r] = mix
        fl_ref[r] = pltpu.roll(s_ref[r, :, 0:LANES], LANES - levels, 1)
        return carry

    lax.fori_loop(1, ext_rows - 1, coef_row, 0)
    qa_ref[...] = s_ref[:, :, 0:LANES]

    def step(src, dst, k):
        def body(r, carry):
            qc = src[r]
            qs = src[r - 1]
            qn = src[r + 1]
            qw = pltpu.roll(qc, 1, 0)
            qe = pltpu.roll(qc, ext_cols - 1, 0)
            horiz = (
                cw_ref[r] * (qw - qc)
                + ce_ref[r] * (qe - qc)
                + cs_ref[r] * (qs - qc)
                + cn_ref[r] * (qn - qc)
            )
            up = pltpu.roll(qc, LANES - 1, 1)
            down = jnp.where(down_ok, mx_ref[r] * (up - qc), 0.0)
            vert = down - pltpu.roll(down, 1, 1)
            updated = qc + wc_ref[r] * (horiz + vert)
            dst[r] = jnp.where(level0, updated + fl_ref[r], updated)
            return carry

        lax.fori_loop(k + 1, ext_rows - 1 - k, body, 0)

    for k in range(SUB):
        if k % 2 == 0:
            step(qa_ref, qb_ref, k)
        else:
            step(qb_ref, qa_ref, k)
    final = qa_ref if SUB % 2 == 0 else qb_ref
    for r in range(rows):
        tile = jnp.transpose(final[width + r, COL_PAD : COL_PAD + cols, :])
        for f in range(o_ref.shape[0]):
            o_ref[f, pl.ds(r, levels, stride=rows), :] = tile[f * HALF : f * HALF + levels]


def run_steps(x, top, bot, left, right, levels, width):
    rows, cols, _ = x.shape
    ext = (rows + 2 * width, cols + 2 * COL_PAD, LANES)
    scratch = [pltpu.VMEM((rows + 2 * width, cols + 2 * COL_PAD, 3 * LANES), jnp.float32)]
    scratch += [pltpu.VMEM(ext, jnp.float32) for _ in range(9)]
    return pl.pallas_call(
        functools.partial(steps_kernel, levels=levels, width=width),
        out_shape=jax.ShapeDtypeStruct((LANES // HALF, levels * rows, cols), jnp.float32),
        scratch_shapes=scratch,
        compiler_params=pltpu.CompilerParams(vmem_limit_bytes=60 * 1024 * 1024),
        interpret=INTERPRET,
    )(x, top, bot, left, right)


def pack_kernel(st_ref, zon_ref, mer_ref, mix_ref, wet_ref, flux_ref, o_ref, t0_ref, t1_ref, t2_ref, *, levels):
    rows = wet_ref.shape[0]
    for t_ref in (t0_ref, t1_ref, t2_ref):
        t_ref[...] = jnp.zeros(t_ref.shape, jnp.float32)
    sub = lax.broadcasted_iota(jnp.int32, (LANES, LANES), 0)

    def body(r, carry):
        levels_at = pl.ds(r, levels, stride=rows)
        t0_ref[0:levels] = st_ref[0, levels_at, :]
        t0_ref[HALF : HALF + levels] = st_ref[1, levels_at, :]
        t1_ref[0:levels] = zon_ref[levels_at, :]
        t1_ref[HALF : HALF + levels] = mer_ref[levels_at, :]
        t2_ref[0:levels] = mix_ref[levels_at, :]
        t2_ref[HALF:LANES] = jnp.broadcast_to(wet_ref[pl.ds(r, 1), :], (LANES - HALF, LANES))
        f0 = jnp.broadcast_to(flux_ref[0, pl.ds(r, 1), :], (LANES, LANES))
        f1 = jnp.broadcast_to(flux_ref[1, pl.ds(r, 1), :], (LANES, LANES))
        t0 = t0_ref[...]
        t0 = jnp.where(sub == levels, f0, t0)
        t0 = jnp.where(sub == HALF + levels, f1, t0)
        o_ref[r, :, 0:LANES] = jnp.transpose(t0)
        o_ref[r, :, LANES : 2 * LANES] = jnp.transpose(t1_ref[...])
        o_ref[r, :, 2 * LANES : 3 * LANES] = jnp.transpose(t2_ref[...])
        return carry

    for r in range(rows):
        body(r, 0)


def pack(tracers, zonal, meridional, mixing, wet, flux):
    fields, levels, rows, cols = tracers.shape
    return pl.pallas_call(
        functools.partial(pack_kernel, levels=levels),
        out_shape=jax.ShapeDtypeStruct((rows, cols, 3 * LANES), jnp.float32),
        scratch_shapes=[pltpu.VMEM((LANES, LANES), jnp.float32) for _ in range(3)],
        interpret=INTERPRET,
    )(
        tracers.reshape(fields, levels * rows, cols),
        zonal.reshape(levels * rows, cols),
        meridional.reshape(levels * rows, cols),
        mixing.reshape(levels * rows, cols),
        wet,
        flux,
    )


def to_lanes(x, fill):
    return jnp.concatenate([jnp.transpose(x, (1, 2, 0)), fill], axis=-1)


def shards(state, zonal, meridional, mixing, exchange_rate, sea_mask, regrid_map):
    tracers = state[0]
    fields, levels, rows, cols = tracers.shape
    section = lax.axis_index("sec")
    sea = sea_mask[0].astype(jnp.float32)
    wet = jnp.where(section == 1, sea, jnp.ones_like(sea))
    surface = tracers[:, 0]
    partner = lax.ppermute(surface, "sec", [(0, 1), (1, 0)])

    regridded = regrid(partner, regrid_map[0])
    flux = exchange_rate[0] * sea * (regridded - surface)

    x = pack(tracers, zonal[0], meridional[0], mixing[0], wet, flux)

    width = SUB
    top = shifted(x[-width:], "lat", 1, cyclic=False)
    bot = shifted(x[:width], "lat", -1, cyclic=False)
    row_block = lax.axis_index("lat")
    wet_lane = lax.broadcasted_iota(jnp.int32, (1, 1, 3 * LANES), 2) >= 2 * LANES + HALF
    top = jnp.where(jnp.logical_and(wet_lane, row_block == 0), 0.0, top)
    bot = jnp.where(jnp.logical_and(wet_lane, row_block == lax.axis_size("lat") - 1), 0.0, bot)
    left = shifted(jnp.concatenate([top[:, -COL_PAD:], x[:, -COL_PAD:], bot[:, -COL_PAD:]], axis=0), "lon", 1)
    right = shifted(jnp.concatenate([top[:, :COL_PAD], x[:, :COL_PAD], bot[:, :COL_PAD]], axis=0), "lon", -1)

    out = run_steps(x, top, bot, left, right, levels, width)
    q = out.reshape(fields, levels, rows, cols)
    return (q[None], flux[None])


def solution(mesh):
    return jax.shard_map(
        shards,
        mesh=mesh,
        in_specs=(
            P("sec", None, None, "lat", "lon"),
            P("sec", None, "lat", "lon"),
            P("sec", None, "lat", "lon"),
            P("sec", None, "lat", "lon"),
            P("sec", "lat", "lon"),
            P("sec", "lat", "lon"),
            P("sec", None, "lat", "lon"),
        ),
        out_specs=(P("sec", None, None, "lat", "lon"), P("sec", None, "lat", "lon")),
        check_vma=False,
    )
```

```python
import functools

import jax
import jax.numpy as jnp
from jax import lax
from jax.experimental import pallas as pl
from jax.experimental.pallas import tpu as pltpu
from jax.sharding import PartitionSpec as P

TAPS = 4
SUB = 4
ROW_REACH = 2
COL_REACH = 3
LANES = 128
HALF = 64
COL_PAD = 8
INTERPRET = False


def shifted(x, axis, step, cyclic=True):
    count = lax.axis_size(axis)
    pairs = [(i, (i + step) % count) for i in range(count) if cyclic or 0 <= i + step < count]
    return lax.ppermute(x, axis, pairs)


def regrid(partner, table):
    fields, rows, cols = partner.shape
    row = lax.broadcasted_iota(jnp.int32, (rows, cols), 0)
    col = lax.broadcasted_iota(jnp.int32, (rows, cols), 1)
    d_row = table // cols - row
    d_col = table % cols - col
    d_col = jnp.where(d_col > cols // 2, d_col - cols, d_col)
    d_col = jnp.where(d_col < -(cols // 2), d_col + cols, d_col)
    padded = jnp.concatenate(
        [jnp.repeat(partner[:, :1], ROW_REACH, axis=1), partner, jnp.repeat(partner[:, -1:], ROW_REACH, axis=1)],
        axis=1,
    )
    moved = {}
    for a in range(-ROW_REACH, ROW_REACH + 1):
        rows_a = padded[:, ROW_REACH + a : ROW_REACH + a + rows]
        for b in range(-COL_REACH, COL_REACH + 1):
            moved[a, b] = jnp.roll(rows_a, -b, axis=2)
    total = None
    for tap in range(TAPS):
        picked = moved[0, 0]
        for (a, b), values in moved.items():
            hit = jnp.logical_and(d_row[tap] == a, d_col[tap] == b)
            picked = jnp.where(hit[None], values, picked)
        total = picked if total is None else total + picked
    return total / TAPS


def steps_kernel(xq_ref, topq_ref, botq_ref, leftq_ref, rightq_ref, xv_ref, topv_ref, botv_ref, leftv_ref, rightv_ref,
                 o_ref, s_ref, qa_ref, qb_ref, cw_ref, ce_ref, cs_ref, cn_ref, wc_ref, mx_ref, fl_ref, wb_ref,
                 *, levels, width):
    rows, cols = xq_ref.shape[0], xq_ref.shape[1]
    ext_rows = rows + 2 * width
    ext_cols = cols + 2 * COL_PAD
    inner = (COL_PAD, COL_PAD + cols)
    for lo, hi, w, x_ref, top_ref, bot_ref, left_ref, right_ref in (
        (0, LANES, width, xq_ref, topq_ref, botq_ref, leftq_ref, rightq_ref),
        (LANES, 3 * LANES, width - 1, xv_ref, topv_ref, botv_ref, leftv_ref, rightv_ref),
    ):
        r0 = width - w
        s_ref[width : width + rows, inner[0] : inner[1], lo:hi] = x_ref[...]
        s_ref[r0:width, inner[0] : inner[1], lo:hi] = top_ref[...]
        s_ref[width + rows : width + rows + w, inner[0] : inner[1], lo:hi] = bot_ref[...]
        s_ref[r0 : width + rows + w, 0:COL_PAD, lo:hi] = left_ref[...]
        s_ref[r0 : width + rows + w, inner[1] :, lo:hi] = right_ref[...]

    lane = lax.broadcasted_iota(jnp.int32, (ext_cols, LANES), 1)
    low = lane < HALF
    level = lane % HALF
    down_ok = level < levels - 1
    level0 = level == 0

    def swap_halves(v):
        return pltpu.roll(v, HALF, 1)

    def wet_row(r, carry):
        spread = jnp.where(lane == levels + 1, s_ref[r, :, 0:LANES], 0.0)
        shift = 1
        while shift < LANES:
            spread = spread + pltpu.roll(spread, shift, 1)
            shift *= 2
        wb_ref[r] = spread
        return carry

    lax.fori_loop(0, ext_rows, wet_row, 0)

    def coef_row(r, carry):
        v1 = s_ref[r, :, LANES : 2 * LANES]
        v2 = s_ref[r, :, 2 * LANES : 3 * LANES]
        zon = jnp.where(low, v1, swap_halves(v1))
        mer = jnp.where(low, swap_halves(v1), v1)
        mix = jnp.where(low, v2, swap_halves(v2))
        wet_c = wb_ref[r]
        wet_s = wb_ref[r - 1]
        wet_n = wb_ref[r + 1]
        wet_w = pltpu.roll(wet_c, 1, 0)
        wet_e = pltpu.roll(wet_c, ext_cols - 1, 0)
        cw_ref[r] = wet_w * jnp.maximum(zon, 0.0)
        ce_ref[r] = wet_e * jnp.maximum(-zon, 0.0)
        cs_ref[r] = wet_s * jnp.maximum(mer, 0.0)
        cn_ref[r] = wet_n * jnp.maximum(-mer, 0.0)
        wc_ref[r] = wet_c
        mx_ref[r] = mix
        fl_ref[r] = pltpu.roll(s_ref[r, :, 0:LANES], LANES - levels, 1)
        return carry

    lax.fori_loop(1, ext_rows - 1, coef_row, 0)
    qa_ref[...] = s_ref[:, :, 0:LANES]

    def step(src, dst, k):
        def body(r, carry):
            qc = src[r]
            qs = src[r - 1]
            qn = src[r + 1]
            qw = pltpu.roll(qc, 1, 0)
            qe = pltpu.roll(qc, ext_cols - 1, 0)
            horiz = (
                cw_ref[r] * (qw - qc)
                + ce_ref[r] * (qe - qc)
                + cs_ref[r] * (qs - qc)
                + cn_ref[r] * (qn - qc)
            )
            up = pltpu.roll(qc, LANES - 1, 1)
            down = jnp.where(down_ok, mx_ref[r] * (up - qc), 0.0)
            vert = down - pltpu.roll(down, 1, 1)
            updated = qc + wc_ref[r] * (horiz + vert)
            dst[r] = jnp.where(level0, updated + fl_ref[r], updated)
            return carry

        lax.fori_loop(k + 1, ext_rows - 1 - k, body, 0)

    for k in range(SUB):
        if k % 2 == 0:
            step(qa_ref, qb_ref, k)
        else:
            step(qb_ref, qa_ref, k)
    final = qa_ref if SUB % 2 == 0 else qb_ref
    for r in range(rows):
        tile = jnp.transpose(final[width + r, inner[0] : inner[1], :])
        for f in range(o_ref.shape[0]):
            o_ref[f, pl.ds(r, levels, stride=rows), :] = tile[f * HALF : f * HALF + levels]


def run_steps(q_parts, v_parts, levels, width):
    rows, cols, _ = q_parts[0].shape
    ext = (rows + 2 * width, cols + 2 * COL_PAD, LANES)
    scratch = [pltpu.VMEM((rows + 2 * width, cols + 2 * COL_PAD, 3 * LANES), jnp.float32)]
    scratch += [pltpu.VMEM(ext, jnp.float32) for _ in range(10)]
    return pl.pallas_call(
        functools.partial(steps_kernel, levels=levels, width=width),
        out_shape=jax.ShapeDtypeStruct((LANES // HALF, levels * rows, cols), jnp.float32),
        scratch_shapes=scratch,
        compiler_params=pltpu.CompilerParams(vmem_limit_bytes=60 * 1024 * 1024),
        interpret=INTERPRET,
    )(*q_parts, *v_parts)


def pack_q_kernel(st_ref, wet_ref, flux_ref, o_ref, t_ref, *, levels):
    rows = wet_ref.shape[0]
    t_ref[...] = jnp.zeros(t_ref.shape, jnp.float32)
    sub = lax.broadcasted_iota(jnp.int32, (LANES, LANES), 0)
    for r in range(rows):
        levels_at = pl.ds(r, levels, stride=rows)
        t_ref[0:levels] = st_ref[0, levels_at, :]
        t_ref[HALF : HALF + levels] = st_ref[1, levels_at, :]
        tile = t_ref[...]
        tile = jnp.where(sub == levels, jnp.broadcast_to(flux_ref[0, pl.ds(r, 1), :], (LANES, LANES)), tile)
        tile = jnp.where(sub == HALF + levels, jnp.broadcast_to(flux_ref[1, pl.ds(r, 1), :], (LANES, LANES)), tile)
        tile = jnp.where(sub == levels + 1, jnp.broadcast_to(wet_ref[pl.ds(r, 1), :], (LANES, LANES)), tile)
        o_ref[r] = jnp.transpose(tile)


def pack_v_kernel(zon_ref, mer_ref, mix_ref, o_ref, t1_ref, t2_ref, *, levels, rows):
    for t_ref in (t1_ref, t2_ref):
        t_ref[...] = jnp.zeros(t_ref.shape, jnp.float32)
    for r in range(rows):
        levels_at = pl.ds(r, levels, stride=rows)
        t1_ref[0:levels] = zon_ref[levels_at, :]
        t1_ref[HALF : HALF + levels] = mer_ref[levels_at, :]
        t2_ref[0:levels] = mix_ref[levels_at, :]
        o_ref[r, :, 0:LANES] = jnp.transpose(t1_ref[...])
        o_ref[r, :, LANES : 2 * LANES] = jnp.transpose(t2_ref[...])


def pack_q(tracers, wet, flux):
    fields, levels, rows, cols = tracers.shape
    return pl.pallas_call(
        functools.partial(pack_q_kernel, levels=levels),
        out_shape=jax.ShapeDtypeStruct((rows, cols, LANES), jnp.float32),
        scratch_shapes=[pltpu.VMEM((LANES, LANES), jnp.float32)],
        interpret=INTERPRET,
    )(tracers.reshape(fields, levels * rows, cols), wet, flux)


def pack_v(zonal, meridional, mixing):
    levels, rows, cols = zonal.shape
    return pl.pallas_call(
        functools.partial(pack_v_kernel, levels=levels, rows=rows),
        out_shape=jax.ShapeDtypeStruct((rows, cols, 2 * LANES), jnp.float32),
        scratch_shapes=[pltpu.VMEM((LANES, LANES), jnp.float32) for _ in range(2)],
        interpret=INTERPRET,
    )(zonal.reshape(levels * rows, cols), meridional.reshape(levels * rows, cols), mixing.reshape(levels * rows, cols))


def halo_parts(x, w, mask=None):
    top = shifted(x[-w:], "lat", 1, cyclic=False)
    bot = shifted(x[:w], "lat", -1, cyclic=False)
    if mask is not None:
        row_block = lax.axis_index("lat")
        top = jnp.where(jnp.logical_and(mask, row_block == 0), 0.0, top)
        bot = jnp.where(jnp.logical_and(mask, row_block == lax.axis_size("lat") - 1), 0.0, bot)
    left = shifted(jnp.concatenate([top[:, -COL_PAD:], x[:, -COL_PAD:], bot[:, -COL_PAD:]], axis=0), "lon", 1)
    right = shifted(jnp.concatenate([top[:, :COL_PAD], x[:, :COL_PAD], bot[:, :COL_PAD]], axis=0), "lon", -1)
    return (x, top, bot, left, right)


def shards(state, zonal, meridional, mixing, exchange_rate, sea_mask, regrid_map):
    tracers = state[0]
    fields, levels, rows, cols = tracers.shape
    width = SUB
    v_parts = halo_parts(pack_v(zonal[0], meridional[0], mixing[0]), width - 1)

    section = lax.axis_index("sec")
    sea = sea_mask[0].astype(jnp.float32)
    wet = jnp.where(section == 1, sea, jnp.ones_like(sea))
    surface = tracers[:, 0]
    partner = lax.ppermute(surface, "sec", [(0, 1), (1, 0)])
    regridded = regrid(partner, regrid_map[0])
    flux = exchange_rate[0] * sea * (regridded - surface)

    wet_lane = lax.broadcasted_iota(jnp.int32, (1, 1, LANES), 2) == levels + 1
    q_parts = halo_parts(pack_q(tracers, wet, flux), width, wet_lane)

    out = run_steps(q_parts, v_parts, levels, width)
    q = out.reshape(fields, levels, rows, cols)
    return (q[None], flux[None])


def solution(mesh):
    return jax.shard_map(
        shards,
        mesh=mesh,
        in_specs=(
            P("sec", None, None, "lat", "lon"),
            P("sec", None, "lat", "lon"),
            P("sec", None, "lat", "lon"),
            P("sec", None, "lat", "lon"),
            P("sec", "lat", "lon"),
            P("sec", "lat", "lon"),
            P("sec", None, "lat", "lon"),
        ),
        out_specs=(P("sec", None, None, "lat", "lon"), P("sec", None, "lat", "lon")),
        check_vma=False,
    )
```

```python
import functools

import jax
import jax.numpy as jnp
from jax import lax
from jax.experimental import pallas as pl
from jax.experimental.pallas import tpu as pltpu
from jax.sharding import PartitionSpec as P

TAPS = 4
SUB = 4
ROW_REACH = 2
COL_REACH = 3
LANES = 128
HALF = 64
COL_PAD = 8
INTERPRET = False


def shifted(x, axis, step, cyclic=True):
    count = lax.axis_size(axis)
    pairs = [(i, (i + step) % count) for i in range(count) if cyclic or 0 <= i + step < count]
    return lax.ppermute(x, axis, pairs)


def regrid(partner, table):
    fields, rows, cols = partner.shape
    row = lax.broadcasted_iota(jnp.int32, (rows, cols), 0)
    col = lax.broadcasted_iota(jnp.int32, (rows, cols), 1)
    d_row = table // cols - row
    d_col = table % cols - col
    d_col = jnp.where(d_col > cols // 2, d_col - cols, d_col)
    d_col = jnp.where(d_col < -(cols // 2), d_col + cols, d_col)
    padded = jnp.concatenate(
        [jnp.repeat(partner[:, :1], ROW_REACH, axis=1), partner, jnp.repeat(partner[:, -1:], ROW_REACH, axis=1)],
        axis=1,
    )
    moved = {}
    for a in range(-ROW_REACH, ROW_REACH + 1):
        rows_a = padded[:, ROW_REACH + a : ROW_REACH + a + rows]
        for b in range(-COL_REACH, COL_REACH + 1):
            moved[a, b] = jnp.roll(rows_a, -b, axis=2)
    total = None
    for tap in range(TAPS):
        picked = moved[0, 0]
        for (a, b), values in moved.items():
            hit = jnp.logical_and(d_row[tap] == a, d_col[tap] == b)
            picked = jnp.where(hit[None], values, picked)
        total = picked if total is None else total + picked
    return total / TAPS


def steps_kernel(xq_ref, topq_ref, botq_ref, leftq_ref, rightq_ref, xv_ref, topv_ref, botv_ref, leftv_ref, rightv_ref,
                 o_ref, s_ref, qa_ref, qb_ref, cw_ref, ce_ref, cs_ref, cn_ref, wc_ref, mx_ref, fl_ref, wb_ref,
                 *, levels, width):
    rows, cols = xq_ref.shape[0], xq_ref.shape[1]
    ext_rows = rows + 2 * width
    ext_cols = cols + 2 * COL_PAD
    inner = (COL_PAD, COL_PAD + cols)
    for lo, hi, w, x_ref, top_ref, bot_ref, left_ref, right_ref in (
        (0, LANES, width, xq_ref, topq_ref, botq_ref, leftq_ref, rightq_ref),
        (LANES, 3 * LANES, width - 1, xv_ref, topv_ref, botv_ref, leftv_ref, rightv_ref),
    ):
        r0 = width - w
        s_ref[width : width + rows, inner[0] : inner[1], lo:hi] = x_ref[...]
        s_ref[r0:width, inner[0] : inner[1], lo:hi] = top_ref[...]
        s_ref[width + rows : width + rows + w, inner[0] : inner[1], lo:hi] = bot_ref[...]
        s_ref[r0 : width + rows + w, 0:COL_PAD, lo:hi] = left_ref[...]
        s_ref[r0 : width + rows + w, inner[1] :, lo:hi] = right_ref[...]

    lane = lax.broadcasted_iota(jnp.int32, (ext_cols, LANES), 1)
    low = lane < HALF
    level = lane % HALF
    down_ok = level < levels - 1
    level0 = level == 0

    def swap_halves(v):
        return pltpu.roll(v, HALF, 1)

    pick = (lax.broadcasted_iota(jnp.int32, (LANES, LANES), 0) == levels + 1).astype(jnp.float32)

    def wet_row(r, carry):
        wb_ref[r] = jnp.dot(s_ref[r, :, 0:LANES], pick, preferred_element_type=jnp.float32)
        return carry

    lax.fori_loop(0, ext_rows, wet_row, 0)

    def coef_row(r, carry):
        v1 = s_ref[r, :, LANES : 2 * LANES]
        v2 = s_ref[r, :, 2 * LANES : 3 * LANES]
        zon = jnp.where(low, v1, swap_halves(v1))
        mer = jnp.where(low, swap_halves(v1), v1)
        mix = jnp.where(low, v2, swap_halves(v2))
        wet_c = wb_ref[r]
        wet_s = wb_ref[r - 1]
        wet_n = wb_ref[r + 1]
        wet_w = pltpu.roll(wet_c, 1, 0)
        wet_e = pltpu.roll(wet_c, ext_cols - 1, 0)
        cw_ref[r] = wet_w * jnp.maximum(zon, 0.0)
        ce_ref[r] = wet_e * jnp.maximum(-zon, 0.0)
        cs_ref[r] = wet_s * jnp.maximum(mer, 0.0)
        cn_ref[r] = wet_n * jnp.maximum(-mer, 0.0)
        wc_ref[r] = wet_c
        mx_ref[r] = mix
        fl_ref[r] = pltpu.roll(s_ref[r, :, 0:LANES], LANES - levels, 1)
        return carry

    lax.fori_loop(1, ext_rows - 1, coef_row, 0)
    qa_ref[...] = s_ref[:, :, 0:LANES]

    def step(src, dst, k):
        def body(r, carry):
            qc = src[r]
            qs = src[r - 1]
            qn = src[r + 1]
            qw = pltpu.roll(qc, 1, 0)
            qe = pltpu.roll(qc, ext_cols - 1, 0)
            horiz = (
                cw_ref[r] * (qw - qc)
                + ce_ref[r] * (qe - qc)
                + cs_ref[r] * (qs - qc)
                + cn_ref[r] * (qn - qc)
            )
            up = pltpu.roll(qc, LANES - 1, 1)
            down = jnp.where(down_ok, mx_ref[r] * (up - qc), 0.0)
            vert = down - pltpu.roll(down, 1, 1)
            updated = qc + wc_ref[r] * (horiz + vert)
            dst[r] = jnp.where(level0, updated + fl_ref[r], updated)
            return carry

        lax.fori_loop(k + 1, ext_rows - 1 - k, body, 0)

    for k in range(SUB):
        if k % 2 == 0:
            step(qa_ref, qb_ref, k)
        else:
            step(qb_ref, qa_ref, k)
    final = qa_ref if SUB % 2 == 0 else qb_ref
    for r in range(rows):
        tile = jnp.transpose(final[width + r, inner[0] : inner[1], :])
        for f in range(o_ref.shape[0]):
            o_ref[f, pl.ds(r, levels, stride=rows), :] = tile[f * HALF : f * HALF + levels]


def run_steps(q_parts, v_parts, levels, width):
    rows, cols, _ = q_parts[0].shape
    ext = (rows + 2 * width, cols + 2 * COL_PAD, LANES)
    scratch = [pltpu.VMEM((rows + 2 * width, cols + 2 * COL_PAD, 3 * LANES), jnp.float32)]
    scratch += [pltpu.VMEM(ext, jnp.float32) for _ in range(10)]
    return pl.pallas_call(
        functools.partial(steps_kernel, levels=levels, width=width),
        out_shape=jax.ShapeDtypeStruct((LANES // HALF, levels * rows, cols), jnp.float32),
        scratch_shapes=scratch,
        compiler_params=pltpu.CompilerParams(vmem_limit_bytes=60 * 1024 * 1024),
        interpret=INTERPRET,
    )(*q_parts, *v_parts)


def pack_q_kernel(st_ref, wet_ref, flux_ref, o_ref, t_ref, *, levels):
    rows = wet_ref.shape[0]
    t_ref[...] = jnp.zeros(t_ref.shape, jnp.float32)
    sub = lax.broadcasted_iota(jnp.int32, (LANES, LANES), 0)
    for r in range(rows):
        levels_at = pl.ds(r, levels, stride=rows)
        t_ref[0:levels] = st_ref[0, levels_at, :]
        t_ref[HALF : HALF + levels] = st_ref[1, levels_at, :]
        tile = t_ref[...]
        tile = jnp.where(sub == levels, jnp.broadcast_to(flux_ref[0, pl.ds(r, 1), :], (LANES, LANES)), tile)
        tile = jnp.where(sub == HALF + levels, jnp.broadcast_to(flux_ref[1, pl.ds(r, 1), :], (LANES, LANES)), tile)
        tile = jnp.where(sub == levels + 1, jnp.broadcast_to(wet_ref[pl.ds(r, 1), :], (LANES, LANES)), tile)
        o_ref[r] = jnp.transpose(tile)


def pack_v_kernel(zon_ref, mer_ref, mix_ref, o_ref, t1_ref, t2_ref, *, levels, rows):
    for t_ref in (t1_ref, t2_ref):
        t_ref[...] = jnp.zeros(t_ref.shape, jnp.float32)
    for r in range(rows):
        levels_at = pl.ds(r, levels, stride=rows)
        t1_ref[0:levels] = zon_ref[levels_at, :]
        t1_ref[HALF : HALF + levels] = mer_ref[levels_at, :]
        t2_ref[0:levels] = mix_ref[levels_at, :]
        o_ref[r, :, 0:LANES] = jnp.transpose(t1_ref[...])
        o_ref[r, :, LANES : 2 * LANES] = jnp.transpose(t2_ref[...])


def pack_q(tracers, wet, flux):
    fields, levels, rows, cols = tracers.shape
    return pl.pallas_call(
        functools.partial(pack_q_kernel, levels=levels),
        out_shape=jax.ShapeDtypeStruct((rows, cols, LANES), jnp.float32),
        scratch_shapes=[pltpu.VMEM((LANES, LANES), jnp.float32)],
        interpret=INTERPRET,
    )(tracers.reshape(fields, levels * rows, cols), wet, flux)


def pack_v(zonal, meridional, mixing):
    levels, rows, cols = zonal.shape
    return pl.pallas_call(
        functools.partial(pack_v_kernel, levels=levels, rows=rows),
        out_shape=jax.ShapeDtypeStruct((rows, cols, 2 * LANES), jnp.float32),
        scratch_shapes=[pltpu.VMEM((LANES, LANES), jnp.float32) for _ in range(2)],
        interpret=INTERPRET,
    )(zonal.reshape(levels * rows, cols), meridional.reshape(levels * rows, cols), mixing.reshape(levels * rows, cols))


def halo_parts(x, w, mask=None):
    top = shifted(x[-w:], "lat", 1, cyclic=False)
    bot = shifted(x[:w], "lat", -1, cyclic=False)
    if mask is not None:
        row_block = lax.axis_index("lat")
        top = jnp.where(jnp.logical_and(mask, row_block == 0), 0.0, top)
        bot = jnp.where(jnp.logical_and(mask, row_block == lax.axis_size("lat") - 1), 0.0, bot)
    left = shifted(jnp.concatenate([top[:, -COL_PAD:], x[:, -COL_PAD:], bot[:, -COL_PAD:]], axis=0), "lon", 1)
    right = shifted(jnp.concatenate([top[:, :COL_PAD], x[:, :COL_PAD], bot[:, :COL_PAD]], axis=0), "lon", -1)
    return (x, top, bot, left, right)


def shards(state, zonal, meridional, mixing, exchange_rate, sea_mask, regrid_map):
    tracers = state[0]
    fields, levels, rows, cols = tracers.shape
    width = SUB
    v_parts = halo_parts(pack_v(zonal[0], meridional[0], mixing[0]), width - 1)

    section = lax.axis_index("sec")
    sea = sea_mask[0].astype(jnp.float32)
    wet = jnp.where(section == 1, sea, jnp.ones_like(sea))
    surface = tracers[:, 0]
    partner = lax.ppermute(surface, "sec", [(0, 1), (1, 0)])
    regridded = regrid(partner, regrid_map[0])
    flux = exchange_rate[0] * sea * (regridded - surface)

    wet_lane = lax.broadcasted_iota(jnp.int32, (1, 1, LANES), 2) == levels + 1
    q_parts = halo_parts(pack_q(tracers, wet, flux), width, wet_lane)

    out = run_steps(q_parts, v_parts, levels, width)
    q = out.reshape(fields, levels, rows, cols)
    return (q[None], flux[None])


def solution(mesh):
    return jax.shard_map(
        shards,
        mesh=mesh,
        in_specs=(
            P("sec", None, None, "lat", "lon"),
            P("sec", None, "lat", "lon"),
            P("sec", None, "lat", "lon"),
            P("sec", None, "lat", "lon"),
            P("sec", "lat", "lon"),
            P("sec", "lat", "lon"),
            P("sec", None, "lat", "lon"),
        ),
        out_specs=(P("sec", None, None, "lat", "lon"), P("sec", None, "lat", "lon")),
        check_vma=False,
    )
```

```python
import functools

import jax
import jax.numpy as jnp
from jax import lax
from jax.experimental import pallas as pl
from jax.experimental.pallas import tpu as pltpu
from jax.sharding import PartitionSpec as P

TAPS = 4
SUB = 4
ROW_REACH = 2
COL_REACH = 3
LANES = 128
HALF = 64
COL_PAD = 8
INTERPRET = False


def shifted(x, axis, step, cyclic=True):
    count = lax.axis_size(axis)
    pairs = [(i, (i + step) % count) for i in range(count) if cyclic or 0 <= i + step < count]
    return lax.ppermute(x, axis, pairs)


def regrid(partner, table):
    fields, rows, cols = partner.shape
    row = lax.broadcasted_iota(jnp.int32, (rows, cols), 0)
    col = lax.broadcasted_iota(jnp.int32, (rows, cols), 1)
    d_row = table // cols - row
    d_col = table % cols - col
    d_col = jnp.where(d_col > cols // 2, d_col - cols, d_col)
    d_col = jnp.where(d_col < -(cols // 2), d_col + cols, d_col)
    padded = jnp.concatenate(
        [jnp.repeat(partner[:, :1], ROW_REACH, axis=1), partner, jnp.repeat(partner[:, -1:], ROW_REACH, axis=1)],
        axis=1,
    )
    moved = {}
    for a in range(-ROW_REACH, ROW_REACH + 1):
        rows_a = padded[:, ROW_REACH + a : ROW_REACH + a + rows]
        for b in range(-COL_REACH, COL_REACH + 1):
            moved[a, b] = jnp.roll(rows_a, -b, axis=2)
    total = None
    for tap in range(TAPS):
        picked = moved[0, 0]
        for (a, b), values in moved.items():
            hit = jnp.logical_and(d_row[tap] == a, d_col[tap] == b)
            picked = jnp.where(hit[None], values, picked)
        total = picked if total is None else total + picked
    return total / TAPS


def steps_kernel(x_ref, top_ref, bot_ref, left_ref, right_ref, o_ref,
                 s_ref, qa_ref, qb_ref, cw_ref, ce_ref, cs_ref, cn_ref, wc_ref, mx_ref, fl_ref, *, levels, width):
    rows, cols = x_ref.shape[0], x_ref.shape[1]
    ext_rows = rows + 2 * width
    ext_cols = cols + 2 * COL_PAD
    s_ref[width : width + rows, COL_PAD : COL_PAD + cols, :] = x_ref[...]
    s_ref[0:width, COL_PAD : COL_PAD + cols, :] = top_ref[...]
    s_ref[width + rows :, COL_PAD : COL_PAD + cols, :] = bot_ref[...]
    s_ref[:, 0:COL_PAD, :] = left_ref[...]
    s_ref[:, COL_PAD + cols :, :] = right_ref[...]

    lane = lax.broadcasted_iota(jnp.int32, (ext_cols, LANES), 1)
    low = lane < HALF
    level = lane % HALF
    down_ok = level < levels - 1
    level0 = level == 0

    def swap_halves(v):
        return pltpu.roll(v, HALF, 1)

    def wet_of(v):
        return jnp.where(low, swap_halves(v), v)

    def coef_row(r, carry):
        v1 = s_ref[r, :, LANES : 2 * LANES]
        v2 = s_ref[r, :, 2 * LANES : 3 * LANES]
        zon = jnp.where(low, v1, swap_halves(v1))
        mer = jnp.where(low, swap_halves(v1), v1)
        mix = jnp.where(low, v2, swap_halves(v2))
        wet_c = wet_of(v2)
        wet_s = wet_of(s_ref[r - 1, :, 2 * LANES : 3 * LANES])
        wet_n = wet_of(s_ref[r + 1, :, 2 * LANES : 3 * LANES])
        wet_w = pltpu.roll(wet_c, 1, 0)
        wet_e = pltpu.roll(wet_c, ext_cols - 1, 0)
        cw_ref[r] = wet_w * jnp.maximum(zon, 0.0)
        ce_ref[r] = wet_e * jnp.maximum(-zon, 0.0)
        cs_ref[r] = wet_s * jnp.maximum(mer, 0.0)
        cn_ref[r] = wet_n * jnp.maximum(-mer, 0.0)
        wc_ref[r] = wet_c
        mx_ref[r] = mix
        fl_ref[r] = pltpu.roll(s_ref[r, :, 0:LANES], LANES - levels, 1)
        return carry

    lax.fori_loop(1, ext_rows - 1, coef_row, 0)
    qa_ref[...] = s_ref[:, :, 0:LANES]

    def step(src, dst, k):
        def body(r, carry):
            qc = src[r]
            qs = src[r - 1]
            qn = src[r + 1]
            qw = pltpu.roll(qc, 1, 0)
            qe = pltpu.roll(qc, ext_cols - 1, 0)
            horiz = (
                cw_ref[r] * (qw - qc)
                + ce_ref[r] * (qe - qc)
                + cs_ref[r] * (qs - qc)
                + cn_ref[r] * (qn - qc)
            )
            up = pltpu.roll(qc, LANES - 1, 1)
            down = jnp.where(down_ok, mx_ref[r] * (up - qc), 0.0)
            vert = down - pltpu.roll(down, 1, 1)
            updated = qc + wc_ref[r] * (horiz + vert)
            dst[r] = jnp.where(level0, updated + fl_ref[r], updated)
            return carry

        lax.fori_loop(k + 1, ext_rows - 1 - k, body, 0)

    for k in range(SUB):
        if k % 2 == 0:
            step(qa_ref, qb_ref, k)
        else:
            step(qb_ref, qa_ref, k)
    final = qa_ref if SUB % 2 == 0 else qb_ref
    for r in range(rows):
        tile = jnp.transpose(final[width + r, COL_PAD : COL_PAD + cols, :])
        for f in range(o_ref.shape[0]):
            o_ref[f, pl.ds(r, levels, stride=rows), :] = tile[f * HALF : f * HALF + levels]


def run_steps(x, top, bot, left, right, levels, width):
    rows, cols, _ = x.shape
    ext = (rows + 2 * width, cols + 2 * COL_PAD, LANES)
    scratch = [pltpu.VMEM((rows + 2 * width, cols + 2 * COL_PAD, 3 * LANES), jnp.float32)]
    scratch += [pltpu.VMEM(ext, jnp.float32) for _ in range(9)]
    return pl.pallas_call(
        functools.partial(steps_kernel, levels=levels, width=width),
        out_shape=jax.ShapeDtypeStruct((LANES // HALF, levels * rows, cols), jnp.float32),
        scratch_shapes=scratch,
        compiler_params=pltpu.CompilerParams(vmem_limit_bytes=60 * 1024 * 1024),
        interpret=INTERPRET,
    )(x, top, bot, left, right)


def pack_kernel(st_ref, zon_ref, mer_ref, mix_ref, wet_ref, flux_ref, o_ref, t0_ref, t1_ref, t2_ref, *, levels):
    rows = wet_ref.shape[0]
    for t_ref in (t0_ref, t1_ref, t2_ref):
        t_ref[...] = jnp.zeros(t_ref.shape, jnp.float32)
    sub = lax.broadcasted_iota(jnp.int32, (LANES, LANES), 0)

    def body(r, carry):
        levels_at = pl.ds(r, levels, stride=rows)
        t0_ref[0:levels] = st_ref[0, levels_at, :]
        t0_ref[HALF : HALF + levels] = st_ref[1, levels_at, :]
        t1_ref[0:levels] = zon_ref[levels_at, :]
        t1_ref[HALF : HALF + levels] = mer_ref[levels_at, :]
        t2_ref[0:levels] = mix_ref[levels_at, :]
        t2_ref[HALF:LANES] = jnp.broadcast_to(wet_ref[pl.ds(r, 1), :], (LANES - HALF, LANES))
        f0 = jnp.broadcast_to(flux_ref[0, pl.ds(r, 1), :], (LANES, LANES))
        f1 = jnp.broadcast_to(flux_ref[1, pl.ds(r, 1), :], (LANES, LANES))
        t0 = t0_ref[...]
        t0 = jnp.where(sub == levels, f0, t0)
        t0 = jnp.where(sub == HALF + levels, f1, t0)
        o_ref[r, :, 0:LANES] = jnp.transpose(t0)
        o_ref[r, :, LANES : 2 * LANES] = jnp.transpose(t1_ref[...])
        o_ref[r, :, 2 * LANES : 3 * LANES] = jnp.transpose(t2_ref[...])
        return carry

    for r in range(rows):
        body(r, 0)


def pack(tracers, zonal, meridional, mixing, wet, flux):
    fields, levels, rows, cols = tracers.shape
    return pl.pallas_call(
        functools.partial(pack_kernel, levels=levels),
        out_shape=jax.ShapeDtypeStruct((rows, cols, 3 * LANES), jnp.float32),
        scratch_shapes=[pltpu.VMEM((LANES, LANES), jnp.float32) for _ in range(3)],
        interpret=INTERPRET,
    )(
        tracers.reshape(fields, levels * rows, cols),
        zonal.reshape(levels * rows, cols),
        meridional.reshape(levels * rows, cols),
        mixing.reshape(levels * rows, cols),
        wet,
        flux,
    )


def to_lanes(x, fill):
    return jnp.concatenate([jnp.transpose(x, (1, 2, 0)), fill], axis=-1)


def shards(state, zonal, meridional, mixing, exchange_rate, sea_mask, regrid_map):
    tracers = state[0]
    fields, levels, rows, cols = tracers.shape
    section = lax.axis_index("sec")
    sea = sea_mask[0].astype(jnp.float32)
    wet = jnp.where(section == 1, sea, jnp.ones_like(sea))
    surface = tracers[:, 0]
    partner = lax.ppermute(surface, "sec", [(0, 1), (1, 0)])

    regridded = regrid(partner, regrid_map[0])
    flux = exchange_rate[0] * sea * (regridded - surface)

    x = pack(tracers, zonal[0], meridional[0], mixing[0], wet, flux)

    width = SUB
    row_block = lax.axis_index("lat")
    wet_lane = lax.broadcasted_iota(jnp.int32, (1, 1, 3 * LANES), 2) >= 2 * LANES + HALF
    top_mask = jnp.logical_and(wet_lane, row_block == 0)
    bot_mask = jnp.logical_and(wet_lane, row_block == lax.axis_size("lat") - 1)
    top = jnp.where(top_mask, 0.0, shifted(x[-width:], "lat", 1, cyclic=False))
    bot = jnp.where(bot_mask, 0.0, shifted(x[:width], "lat", -1, cyclic=False))
    left = shifted(x[:, -COL_PAD:], "lon", 1)
    right = shifted(x[:, :COL_PAD], "lon", -1)
    upper = jnp.where(top_mask, 0.0, shifted(jnp.concatenate([left[-width:], right[-width:]], axis=1), "lat", 1, cyclic=False))
    lower = jnp.where(bot_mask, 0.0, shifted(jnp.concatenate([left[:width], right[:width]], axis=1), "lat", -1, cyclic=False))
    left = jnp.concatenate([upper[:, :COL_PAD], left, lower[:, :COL_PAD]], axis=0)
    right = jnp.concatenate([upper[:, COL_PAD:], right, lower[:, COL_PAD:]], axis=0)

    out = run_steps(x, top, bot, left, right, levels, width)
    q = out.reshape(fields, levels, rows, cols)
    return (q[None], flux[None])


def solution(mesh):
    return jax.shard_map(
        shards,
        mesh=mesh,
        in_specs=(
            P("sec", None, None, "lat", "lon"),
            P("sec", None, "lat", "lon"),
            P("sec", None, "lat", "lon"),
            P("sec", None, "lat", "lon"),
            P("sec", "lat", "lon"),
            P("sec", "lat", "lon"),
            P("sec", None, "lat", "lon"),
        ),
        out_specs=(P("sec", None, None, "lat", "lon"), P("sec", None, "lat", "lon")),
        check_vma=False,
    )
```

```python
import functools

import jax
import jax.numpy as jnp
from jax import lax
from jax.experimental import pallas as pl
from jax.experimental.pallas import tpu as pltpu
from jax.sharding import PartitionSpec as P

TAPS = 4
SUB = 4
ROW_REACH = 2
COL_REACH = 3
LANES = 128
HALF = 64
COL_PAD = 8
INTERPRET = False


def shifted(x, axis, step, cyclic=True):
    count = lax.axis_size(axis)
    pairs = [(i, (i + step) % count) for i in range(count) if cyclic or 0 <= i + step < count]
    return lax.ppermute(x, axis, pairs)


def regrid(partner, table):
    fields, rows, cols = partner.shape
    row = lax.broadcasted_iota(jnp.int32, (rows, cols), 0)
    col = lax.broadcasted_iota(jnp.int32, (rows, cols), 1)
    d_row = table // cols - row
    d_col = table % cols - col
    d_col = jnp.where(d_col > cols // 2, d_col - cols, d_col)
    d_col = jnp.where(d_col < -(cols // 2), d_col + cols, d_col)
    padded = jnp.concatenate(
        [jnp.repeat(partner[:, :1], ROW_REACH, axis=1), partner, jnp.repeat(partner[:, -1:], ROW_REACH, axis=1)],
        axis=1,
    )
    moved = {}
    for a in range(-ROW_REACH, ROW_REACH + 1):
        rows_a = padded[:, ROW_REACH + a : ROW_REACH + a + rows]
        for b in range(-COL_REACH, COL_REACH + 1):
            moved[a, b] = jnp.roll(rows_a, -b, axis=2)
    total = None
    for tap in range(TAPS):
        picked = moved[0, 0]
        for (a, b), values in moved.items():
            hit = jnp.logical_and(d_row[tap] == a, d_col[tap] == b)
            picked = jnp.where(hit[None], values, picked)
        total = picked if total is None else total + picked
    return total / TAPS


def steps_kernel(x_ref, top_ref, bot_ref, left_ref, right_ref, o_ref,
                 s_ref, qa_ref, qb_ref, cw_ref, ce_ref, cs_ref, cn_ref, wc_ref, mx_ref, fl_ref, *, levels, width):
    rows, cols = x_ref.shape[0], x_ref.shape[1]
    ext_rows = rows + 2 * width
    ext_cols = cols + 2 * COL_PAD
    s_ref[width : width + rows, COL_PAD : COL_PAD + cols, :] = x_ref[...]
    s_ref[0:width, COL_PAD : COL_PAD + cols, :] = top_ref[...]
    s_ref[width + rows :, COL_PAD : COL_PAD + cols, :] = bot_ref[...]
    s_ref[:, 0:COL_PAD, :] = left_ref[...]
    s_ref[:, COL_PAD + cols :, :] = right_ref[...]

    lane = lax.broadcasted_iota(jnp.int32, (ext_cols, LANES), 1)
    low = lane < HALF
    level = lane % HALF
    down_ok = level < levels - 1
    level0 = level == 0

    def swap_halves(v):
        return pltpu.roll(v, HALF, 1)

    def wet_of(v):
        return jnp.where(low, swap_halves(v), v)

    def coef_row(r, carry):
        v1 = s_ref[r, :, LANES : 2 * LANES]
        v2 = s_ref[r, :, 2 * LANES : 3 * LANES]
        zon = jnp.where(low, v1, swap_halves(v1))
        mer = jnp.where(low, swap_halves(v1), v1)
        mix = jnp.where(low, v2, swap_halves(v2))
        wet_c = wet_of(v2)
        wet_s = wet_of(s_ref[r - 1, :, 2 * LANES : 3 * LANES])
        wet_n = wet_of(s_ref[r + 1, :, 2 * LANES : 3 * LANES])
        wet_w = pltpu.roll(wet_c, 1, 0)
        wet_e = pltpu.roll(wet_c, ext_cols - 1, 0)
        cw_ref[r] = wet_w * jnp.maximum(zon, 0.0)
        ce_ref[r] = wet_e * jnp.maximum(-zon, 0.0)
        cs_ref[r] = wet_s * jnp.maximum(mer, 0.0)
        cn_ref[r] = wet_n * jnp.maximum(-mer, 0.0)
        wc_ref[r] = wet_c
        mx_ref[r] = mix
        fl_ref[r] = pltpu.roll(s_ref[r, :, 0:LANES], LANES - levels, 1)
        return carry

    lax.fori_loop(1, ext_rows - 1, coef_row, 0)
    qa_ref[...] = s_ref[:, :, 0:LANES]

    def step(src, dst, k):
        def body(r, carry):
            qc = src[r]
            qs = src[r - 1]
            qn = src[r + 1]
            qw = pltpu.roll(qc, 1, 0)
            qe = pltpu.roll(qc, ext_cols - 1, 0)
            horiz = (
                cw_ref[r] * (qw - qc)
                + ce_ref[r] * (qe - qc)
                + cs_ref[r] * (qs - qc)
                + cn_ref[r] * (qn - qc)
            )
            up = pltpu.roll(qc, LANES - 1, 1)
            down = jnp.where(down_ok, mx_ref[r] * (up - qc), 0.0)
            vert = down - pltpu.roll(down, 1, 1)
            updated = qc + wc_ref[r] * (horiz + vert)
            dst[r] = jnp.where(level0, updated + fl_ref[r], updated)
            return carry

        lax.fori_loop(k + 1, ext_rows - 1 - k, body, 0)

    for k in range(SUB):
        if k % 2 == 0:
            step(qa_ref, qb_ref, k)
        else:
            step(qb_ref, qa_ref, k)
    final = qa_ref if SUB % 2 == 0 else qb_ref
    for r in range(rows):
        tile = jnp.transpose(final[width + r, COL_PAD : COL_PAD + cols, :])
        for f in range(o_ref.shape[0]):
            o_ref[f, pl.ds(r, levels, stride=rows), :] = tile[f * HALF : f * HALF + levels]


def run_steps(x, top, bot, left, right, levels, width):
    rows, cols, _ = x.shape
    ext = (rows + 2 * width, cols + 2 * COL_PAD, LANES)
    scratch = [pltpu.VMEM((rows + 2 * width, cols + 2 * COL_PAD, 3 * LANES), jnp.float32)]
    scratch += [pltpu.VMEM(ext, jnp.float32) for _ in range(9)]
    return pl.pallas_call(
        functools.partial(steps_kernel, levels=levels, width=width),
        out_shape=jax.ShapeDtypeStruct((LANES // HALF, levels * rows, cols), jnp.float32),
        scratch_shapes=scratch,
        compiler_params=pltpu.CompilerParams(vmem_limit_bytes=60 * 1024 * 1024),
        interpret=INTERPRET,
    )(x, top, bot, left, right)


def pack_kernel(st_ref, zon_ref, mer_ref, mix_ref, wet_ref, flux_ref, o_ref, last_ref, first_ref, east_ref, west_ref,
                t0_ref, t1_ref, t2_ref, *, levels, width):
    rows = wet_ref.shape[0]
    for t_ref in (t0_ref, t1_ref, t2_ref):
        t_ref[...] = jnp.zeros(t_ref.shape, jnp.float32)
    sub = lax.broadcasted_iota(jnp.int32, (LANES, LANES), 0)

    def body(r, carry):
        levels_at = pl.ds(r, levels, stride=rows)
        t0_ref[0:levels] = st_ref[0, levels_at, :]
        t0_ref[HALF : HALF + levels] = st_ref[1, levels_at, :]
        t1_ref[0:levels] = zon_ref[levels_at, :]
        t1_ref[HALF : HALF + levels] = mer_ref[levels_at, :]
        t2_ref[0:levels] = mix_ref[levels_at, :]
        t2_ref[HALF:LANES] = jnp.broadcast_to(wet_ref[pl.ds(r, 1), :], (LANES - HALF, LANES))
        f0 = jnp.broadcast_to(flux_ref[0, pl.ds(r, 1), :], (LANES, LANES))
        f1 = jnp.broadcast_to(flux_ref[1, pl.ds(r, 1), :], (LANES, LANES))
        t0 = t0_ref[...]
        t0 = jnp.where(sub == levels, f0, t0)
        t0 = jnp.where(sub == HALF + levels, f1, t0)
        for b, tile in enumerate((t0, t1_ref[...], t2_ref[...])):
            lanes = slice(b * LANES, (b + 1) * LANES)
            cell = jnp.transpose(tile)
            o_ref[r, :, lanes] = cell
            if r >= rows - width:
                last_ref[r - (rows - width), :, lanes] = cell
            if r < width:
                first_ref[r, :, lanes] = cell
            east_ref[r, :, lanes] = cell[-COL_PAD:]
            west_ref[r, :, lanes] = cell[:COL_PAD]
        return carry

    for r in range(rows):
        body(r, 0)


def pack(tracers, zonal, meridional, mixing, wet, flux, width):
    fields, levels, rows, cols = tracers.shape
    return pl.pallas_call(
        functools.partial(pack_kernel, levels=levels, width=width),
        out_shape=(
            jax.ShapeDtypeStruct((rows, cols, 3 * LANES), jnp.float32),
            jax.ShapeDtypeStruct((width, cols, 3 * LANES), jnp.float32),
            jax.ShapeDtypeStruct((width, cols, 3 * LANES), jnp.float32),
            jax.ShapeDtypeStruct((rows, COL_PAD, 3 * LANES), jnp.float32),
            jax.ShapeDtypeStruct((rows, COL_PAD, 3 * LANES), jnp.float32),
        ),
        scratch_shapes=[pltpu.VMEM((LANES, LANES), jnp.float32) for _ in range(3)],
        interpret=INTERPRET,
    )(
        tracers.reshape(fields, levels * rows, cols),
        zonal.reshape(levels * rows, cols),
        meridional.reshape(levels * rows, cols),
        mixing.reshape(levels * rows, cols),
        wet,
        flux,
    )


def to_lanes(x, fill):
    return jnp.concatenate([jnp.transpose(x, (1, 2, 0)), fill], axis=-1)


def shards(state, zonal, meridional, mixing, exchange_rate, sea_mask, regrid_map):
    tracers = state[0]
    fields, levels, rows, cols = tracers.shape
    section = lax.axis_index("sec")
    sea = sea_mask[0].astype(jnp.float32)
    wet = jnp.where(section == 1, sea, jnp.ones_like(sea))
    surface = tracers[:, 0]
    partner = lax.ppermute(surface, "sec", [(0, 1), (1, 0)])

    regridded = regrid(partner, regrid_map[0])
    flux = exchange_rate[0] * sea * (regridded - surface)

    width = SUB
    x, last, first, east, west = pack(tracers, zonal[0], meridional[0], mixing[0], wet, flux, width)

    row_block = lax.axis_index("lat")
    wet_lane = lax.broadcasted_iota(jnp.int32, (1, 1, 3 * LANES), 2) >= 2 * LANES + HALF
    top_mask = jnp.logical_and(wet_lane, row_block == 0)
    bot_mask = jnp.logical_and(wet_lane, row_block == lax.axis_size("lat") - 1)
    top = jnp.where(top_mask, 0.0, shifted(last, "lat", 1, cyclic=False))
    bot = jnp.where(bot_mask, 0.0, shifted(first, "lat", -1, cyclic=False))
    left = shifted(east, "lon", 1)
    right = shifted(west, "lon", -1)
    upper = jnp.where(top_mask, 0.0, shifted(jnp.concatenate([left[-width:], right[-width:]], axis=1), "lat", 1, cyclic=False))
    lower = jnp.where(bot_mask, 0.0, shifted(jnp.concatenate([left[:width], right[:width]], axis=1), "lat", -1, cyclic=False))
    left = jnp.concatenate([upper[:, :COL_PAD], left, lower[:, :COL_PAD]], axis=0)
    right = jnp.concatenate([upper[:, COL_PAD:], right, lower[:, COL_PAD:]], axis=0)

    out = run_steps(x, top, bot, left, right, levels, width)
    q = out.reshape(fields, levels, rows, cols)
    return (q[None], flux[None])


def solution(mesh):
    return jax.shard_map(
        shards,
        mesh=mesh,
        in_specs=(
            P("sec", None, None, "lat", "lon"),
            P("sec", None, "lat", "lon"),
            P("sec", None, "lat", "lon"),
            P("sec", None, "lat", "lon"),
            P("sec", "lat", "lon"),
            P("sec", "lat", "lon"),
            P("sec", None, "lat", "lon"),
        ),
        out_specs=(P("sec", None, None, "lat", "lon"), P("sec", None, "lat", "lon")),
        check_vma=False,
    )
```

```python
import functools

import jax
import jax.numpy as jnp
from jax import lax
from jax.experimental import pallas as pl
from jax.experimental.pallas import tpu as pltpu
from jax.sharding import PartitionSpec as P

TAPS = 4
SUB = 4
ROW_REACH = 2
COL_REACH = 3
LANES = 128
HALF = 64
COL_PAD = 8
INTERPRET = False


def shifted(x, axis, step, cyclic=True):
    count = lax.axis_size(axis)
    pairs = [(i, (i + step) % count) for i in range(count) if cyclic or 0 <= i + step < count]
    return lax.ppermute(x, axis, pairs)


def regrid(partner, table):
    fields, rows, cols = partner.shape
    row = lax.broadcasted_iota(jnp.int32, (rows, cols), 0)
    col = lax.broadcasted_iota(jnp.int32, (rows, cols), 1)
    d_row = table // cols - row
    d_col = table % cols - col
    d_col = jnp.where(d_col > cols // 2, d_col - cols, d_col)
    d_col = jnp.where(d_col < -(cols // 2), d_col + cols, d_col)
    padded = jnp.concatenate(
        [jnp.repeat(partner[:, :1], ROW_REACH, axis=1), partner, jnp.repeat(partner[:, -1:], ROW_REACH, axis=1)],
        axis=1,
    )
    moved = {}
    for a in range(-ROW_REACH, ROW_REACH + 1):
        rows_a = padded[:, ROW_REACH + a : ROW_REACH + a + rows]
        for b in range(-COL_REACH, COL_REACH + 1):
            moved[a, b] = jnp.roll(rows_a, -b, axis=2)
    total = None
    for tap in range(TAPS):
        picked = moved[0, 0]
        for (a, b), values in moved.items():
            hit = jnp.logical_and(d_row[tap] == a, d_col[tap] == b)
            picked = jnp.where(hit[None], values, picked)
        total = picked if total is None else total + picked
    return total / TAPS


def steps_kernel(x_ref, top_ref, bot_ref, left_ref, right_ref, o_ref,
                 s_ref, qa_ref, qb_ref, cw_ref, ce_ref, cs_ref, cn_ref, wc_ref, mx_ref, fl_ref, *, levels, width):
    rows, cols = x_ref.shape[0], x_ref.shape[1]
    ext_rows = rows + 2 * width
    ext_cols = cols + 2 * COL_PAD
    s_ref[width : width + rows, COL_PAD : COL_PAD + cols, :] = x_ref[...]
    s_ref[0:width, COL_PAD : COL_PAD + cols, :] = top_ref[...]
    s_ref[width + rows :, COL_PAD : COL_PAD + cols, :] = bot_ref[...]
    s_ref[:, 0:COL_PAD, :] = left_ref[...]
    s_ref[:, COL_PAD + cols :, :] = right_ref[...]

    lane = lax.broadcasted_iota(jnp.int32, (ext_cols, LANES), 1)
    low = lane < HALF
    level = lane % HALF
    down_ok = level < levels - 1
    level0 = level == 0

    def swap_halves(v):
        return pltpu.roll(v, HALF, 1)

    def wet_of(v):
        return jnp.where(low, swap_halves(v), v)

    def coef_row(r, carry):
        v1 = s_ref[r, :, LANES : 2 * LANES]
        v2 = s_ref[r, :, 2 * LANES : 3 * LANES]
        zon = jnp.where(low, v1, swap_halves(v1))
        mer = jnp.where(low, swap_halves(v1), v1)
        mix = jnp.where(low, v2, swap_halves(v2))
        wet_c = wet_of(v2)
        wet_s = wet_of(s_ref[r - 1, :, 2 * LANES : 3 * LANES])
        wet_n = wet_of(s_ref[r + 1, :, 2 * LANES : 3 * LANES])
        wet_w = pltpu.roll(wet_c, 1, 0)
        wet_e = pltpu.roll(wet_c, ext_cols - 1, 0)
        cw_ref[r] = wet_w * jnp.maximum(zon, 0.0)
        ce_ref[r] = wet_e * jnp.maximum(-zon, 0.0)
        cs_ref[r] = wet_s * jnp.maximum(mer, 0.0)
        cn_ref[r] = wet_n * jnp.maximum(-mer, 0.0)
        wc_ref[r] = wet_c
        mx_ref[r] = mix
        fl_ref[r] = pltpu.roll(s_ref[r, :, 0:LANES], LANES - levels, 1)
        return carry

    lax.fori_loop(1, ext_rows - 1, coef_row, 0)
    qa_ref[...] = s_ref[:, :, 0:LANES]

    def step(src, dst, k):
        def body(r, carry):
            qc = src[r]
            qs = src[r - 1]
            qn = src[r + 1]
            qw = pltpu.roll(qc, 1, 0)
            qe = pltpu.roll(qc, ext_cols - 1, 0)
            horiz = (
                cw_ref[r] * (qw - qc)
                + ce_ref[r] * (qe - qc)
                + cs_ref[r] * (qs - qc)
                + cn_ref[r] * (qn - qc)
            )
            up = pltpu.roll(qc, LANES - 1, 1)
            down = jnp.where(down_ok, mx_ref[r] * (up - qc), 0.0)
            vert = down - pltpu.roll(down, 1, 1)
            updated = qc + wc_ref[r] * (horiz + vert)
            dst[r] = jnp.where(level0, updated + fl_ref[r], updated)
            return carry

        lax.fori_loop(k + 1, ext_rows - 1 - k, body, 0)

    for k in range(SUB):
        if k % 2 == 0:
            step(qa_ref, qb_ref, k)
        else:
            step(qb_ref, qa_ref, k)
    final = qa_ref if SUB % 2 == 0 else qb_ref
    for r in range(rows):
        tile = jnp.transpose(final[width + r, COL_PAD : COL_PAD + cols, :])
        for f in range(o_ref.shape[0]):
            o_ref[f, pl.ds(r, levels, stride=rows), :] = tile[f * HALF : f * HALF + levels]


def run_steps(x, top, bot, left, right, levels, width):
    rows, cols, _ = x.shape
    ext = (rows + 2 * width, cols + 2 * COL_PAD, LANES)
    scratch = [pltpu.VMEM((rows + 2 * width, cols + 2 * COL_PAD, 3 * LANES), jnp.float32)]
    scratch += [pltpu.VMEM(ext, jnp.float32) for _ in range(9)]
    return pl.pallas_call(
        functools.partial(steps_kernel, levels=levels, width=width),
        out_shape=jax.ShapeDtypeStruct((LANES // HALF, levels * rows, cols), jnp.float32),
        scratch_shapes=scratch,
        compiler_params=pltpu.CompilerParams(vmem_limit_bytes=60 * 1024 * 1024),
        interpret=INTERPRET,
    )(x, top, bot, left, right)


def pack_kernel(st_ref, zon_ref, mer_ref, mix_ref, wet_ref, flux_ref, o_ref, t0_ref, t1_ref, t2_ref, *, levels):
    rows = wet_ref.shape[0]
    for t_ref in (t0_ref, t1_ref, t2_ref):
        t_ref[...] = jnp.zeros(t_ref.shape, jnp.float32)
    sub = lax.broadcasted_iota(jnp.int32, (LANES, LANES), 0)

    def body(r, carry):
        levels_at = pl.ds(r, levels, stride=rows)
        t0_ref[0:levels] = st_ref[0, levels_at, :]
        t0_ref[HALF : HALF + levels] = st_ref[1, levels_at, :]
        t1_ref[0:levels] = zon_ref[levels_at, :]
        t1_ref[HALF : HALF + levels] = mer_ref[levels_at, :]
        t2_ref[0:levels] = mix_ref[levels_at, :]
        t2_ref[HALF:LANES] = jnp.broadcast_to(wet_ref[pl.ds(r, 1), :], (LANES - HALF, LANES))
        f0 = jnp.broadcast_to(flux_ref[0, pl.ds(r, 1), :], (LANES, LANES))
        f1 = jnp.broadcast_to(flux_ref[1, pl.ds(r, 1), :], (LANES, LANES))
        t0 = t0_ref[...]
        t0 = jnp.where(sub == levels, f0, t0)
        t0 = jnp.where(sub == HALF + levels, f1, t0)
        o_ref[r, :, 0:LANES] = jnp.transpose(t0)
        o_ref[r, :, LANES : 2 * LANES] = jnp.transpose(t1_ref[...])
        o_ref[r, :, 2 * LANES : 3 * LANES] = jnp.transpose(t2_ref[...])
        return carry

    for r in range(rows):
        body(r, 0)


def pack(tracers, zonal, meridional, mixing, wet, flux):
    fields, levels, rows, cols = tracers.shape
    return pl.pallas_call(
        functools.partial(pack_kernel, levels=levels),
        out_shape=jax.ShapeDtypeStruct((rows, cols, 3 * LANES), jnp.float32),
        scratch_shapes=[pltpu.VMEM((LANES, LANES), jnp.float32) for _ in range(3)],
        interpret=INTERPRET,
    )(
        tracers.reshape(fields, levels * rows, cols),
        zonal.reshape(levels * rows, cols),
        meridional.reshape(levels * rows, cols),
        mixing.reshape(levels * rows, cols),
        wet,
        flux,
    )


def to_lanes(x, fill):
    return jnp.concatenate([jnp.transpose(x, (1, 2, 0)), fill], axis=-1)


def shards(state, zonal, meridional, mixing, exchange_rate, sea_mask, regrid_map):
    tracers = state[0]
    fields, levels, rows, cols = tracers.shape
    section = lax.axis_index("sec")
    sea = sea_mask[0].astype(jnp.float32)
    wet = jnp.where(section == 1, sea, jnp.ones_like(sea))
    surface = tracers[:, 0]
    partner = lax.ppermute(surface, "sec", [(0, 1), (1, 0)])

    regridded = regrid(partner, regrid_map[0])
    flux = exchange_rate[0] * sea * (regridded - surface)

    x = pack(tracers, zonal[0], meridional[0], mixing[0], wet, flux)

    width = SUB
    row_block = lax.axis_index("lat")
    wet_lane = lax.broadcasted_iota(jnp.int32, (1, 1, 3 * LANES), 2) >= 2 * LANES + HALF
    top_mask = jnp.logical_and(wet_lane, row_block == 0)
    bot_mask = jnp.logical_and(wet_lane, row_block == lax.axis_size("lat") - 1)
    top = jnp.where(top_mask, 0.0, shifted(x[-width:], "lat", 1, cyclic=False))
    bot = jnp.where(bot_mask, 0.0, shifted(x[:width], "lat", -1, cyclic=False))
    left = shifted(x[:, -COL_PAD:], "lon", 1)
    right = shifted(x[:, :COL_PAD], "lon", -1)
    east = shifted(jnp.concatenate([top[:, -COL_PAD:], bot[:, -COL_PAD:]], axis=0), "lon", 1)
    west = shifted(jnp.concatenate([top[:, :COL_PAD], bot[:, :COL_PAD]], axis=0), "lon", -1)
    left = jnp.concatenate([east[:width], left, east[width:]], axis=0)
    right = jnp.concatenate([west[:width], right, west[width:]], axis=0)

    out = run_steps(x, top, bot, left, right, levels, width)
    q = out.reshape(fields, levels, rows, cols)
    return (q[None], flux[None])


def solution(mesh):
    return jax.shard_map(
        shards,
        mesh=mesh,
        in_specs=(
            P("sec", None, None, "lat", "lon"),
            P("sec", None, "lat", "lon"),
            P("sec", None, "lat", "lon"),
            P("sec", None, "lat", "lon"),
            P("sec", "lat", "lon"),
            P("sec", "lat", "lon"),
            P("sec", None, "lat", "lon"),
        ),
        out_specs=(P("sec", None, None, "lat", "lon"), P("sec", None, "lat", "lon")),
        check_vma=False,
    )
```

```python
import functools

import jax
import jax.numpy as jnp
from jax import lax
from jax.experimental import pallas as pl
from jax.experimental.pallas import tpu as pltpu
from jax.sharding import PartitionSpec as P

TAPS = 4
SUB = 4
ROW_REACH = 2
COL_REACH = 3
LANES = 128
HALF = 64
COL_PAD = 8
INTERPRET = False


def shifted(x, axis, step, cyclic=True):
    count = lax.axis_size(axis)
    pairs = [(i, (i + step) % count) for i in range(count) if cyclic or 0 <= i + step < count]
    return lax.ppermute(x, axis, pairs)


def regrid(partner, table):
    fields, rows, cols = partner.shape
    row = lax.broadcasted_iota(jnp.int32, (rows, cols), 0)
    col = lax.broadcasted_iota(jnp.int32, (rows, cols), 1)
    d_row = table // cols - row
    d_col = table % cols - col
    d_col = jnp.where(d_col > cols // 2, d_col - cols, d_col)
    d_col = jnp.where(d_col < -(cols // 2), d_col + cols, d_col)
    padded = jnp.concatenate(
        [jnp.repeat(partner[:, :1], ROW_REACH, axis=1), partner, jnp.repeat(partner[:, -1:], ROW_REACH, axis=1)],
        axis=1,
    )
    moved = {}
    for a in range(-ROW_REACH, ROW_REACH + 1):
        rows_a = padded[:, ROW_REACH + a : ROW_REACH + a + rows]
        for b in range(-COL_REACH, COL_REACH + 1):
            moved[a, b] = jnp.roll(rows_a, -b, axis=2)
    total = None
    for tap in range(TAPS):
        picked = moved[0, 0]
        for (a, b), values in moved.items():
            hit = jnp.logical_and(d_row[tap] == a, d_col[tap] == b)
            picked = jnp.where(hit[None], values, picked)
        total = picked if total is None else total + picked
    return total / TAPS


def steps_kernel(x_ref, top_ref, bot_ref, left_ref, right_ref, o_ref,
                 s_ref, qa_ref, qb_ref, cw_ref, ce_ref, cs_ref, cn_ref, wc_ref, mx_ref, fl_ref, *, levels, width):
    rows, cols = x_ref.shape[0], x_ref.shape[1]
    ext_rows = rows + 2 * width
    ext_cols = cols + 2 * COL_PAD
    s_ref[width : width + rows, COL_PAD : COL_PAD + cols, :] = x_ref[...]
    s_ref[0:width, COL_PAD : COL_PAD + cols, :] = top_ref[...]
    s_ref[width + rows :, COL_PAD : COL_PAD + cols, :] = bot_ref[...]
    s_ref[:, 0:COL_PAD, :] = left_ref[...]
    s_ref[:, COL_PAD + cols :, :] = right_ref[...]

    lane = lax.broadcasted_iota(jnp.int32, (ext_cols, LANES), 1)
    low = lane < HALF
    level = lane % HALF
    down_ok = level < levels - 1
    level0 = level == 0

    def swap_halves(v):
        return pltpu.roll(v, HALF, 1)

    def wet_of(v):
        return jnp.where(low, swap_halves(v), v)

    def coef_row(r, carry):
        v1 = s_ref[r, :, LANES : 2 * LANES]
        v2 = s_ref[r, :, 2 * LANES : 3 * LANES]
        zon = jnp.where(low, v1, swap_halves(v1))
        mer = jnp.where(low, swap_halves(v1), v1)
        mix = jnp.where(low, v2, swap_halves(v2))
        wet_c = wet_of(v2)
        wet_s = wet_of(s_ref[r - 1, :, 2 * LANES : 3 * LANES])
        wet_n = wet_of(s_ref[r + 1, :, 2 * LANES : 3 * LANES])
        wet_w = pltpu.roll(wet_c, 1, 0)
        wet_e = pltpu.roll(wet_c, ext_cols - 1, 0)
        cw_ref[r] = wet_w * jnp.maximum(zon, 0.0)
        ce_ref[r] = wet_e * jnp.maximum(-zon, 0.0)
        cs_ref[r] = wet_s * jnp.maximum(mer, 0.0)
        cn_ref[r] = wet_n * jnp.maximum(-mer, 0.0)
        wc_ref[r] = wet_c
        mx_ref[r] = mix
        fl_ref[r] = pltpu.roll(s_ref[r, :, 0:LANES], LANES - levels, 1)
        return carry

    lax.fori_loop(1, ext_rows - 1, coef_row, 0)
    qa_ref[...] = s_ref[:, :, 0:LANES]

    def step(src, dst, k):
        def body(r, carry):
            qc = src[r]
            qs = src[r - 1]
            qn = src[r + 1]
            qw = pltpu.roll(qc, 1, 0)
            qe = pltpu.roll(qc, ext_cols - 1, 0)
            horiz = (
                cw_ref[r] * (qw - qc)
                + ce_ref[r] * (qe - qc)
                + cs_ref[r] * (qs - qc)
                + cn_ref[r] * (qn - qc)
            )
            up = pltpu.roll(qc, LANES - 1, 1)
            down = jnp.where(down_ok, mx_ref[r] * (up - qc), 0.0)
            vert = down - pltpu.roll(down, 1, 1)
            updated = qc + wc_ref[r] * (horiz + vert)
            dst[r] = jnp.where(level0, updated + fl_ref[r], updated)
            return carry

        lax.fori_loop(k + 1, ext_rows - 1 - k, body, 0)

    for k in range(SUB):
        if k % 2 == 0:
            step(qa_ref, qb_ref, k)
        else:
            step(qb_ref, qa_ref, k)
    final = qa_ref if SUB % 2 == 0 else qb_ref
    for r in range(rows):
        tile = jnp.transpose(final[width + r, COL_PAD : COL_PAD + cols, :])
        for f in range(o_ref.shape[0]):
            o_ref[f, pl.ds(r, levels, stride=rows), :] = tile[f * HALF : f * HALF + levels]


def run_steps(x, top, bot, left, right, levels, width):
    rows, cols, _ = x.shape
    ext = (rows + 2 * width, cols + 2 * COL_PAD, LANES)
    scratch = [pltpu.VMEM((rows + 2 * width, cols + 2 * COL_PAD, 3 * LANES), jnp.float32)]
    scratch += [pltpu.VMEM(ext, jnp.float32) for _ in range(9)]
    return pl.pallas_call(
        functools.partial(steps_kernel, levels=levels, width=width),
        out_shape=jax.ShapeDtypeStruct((LANES // HALF, levels * rows, cols), jnp.float32),
        scratch_shapes=scratch,
        compiler_params=pltpu.CompilerParams(vmem_limit_bytes=60 * 1024 * 1024),
        interpret=INTERPRET,
    )(x, top, bot, left, right)


def pack_kernel(st_ref, zon_ref, mer_ref, mix_ref, wet_ref, flux_ref, o_ref, t0_ref, t1_ref, t2_ref, *, levels):
    rows = wet_ref.shape[0]
    for t_ref in (t0_ref, t1_ref, t2_ref):
        t_ref[...] = jnp.zeros(t_ref.shape, jnp.float32)
    sub = lax.broadcasted_iota(jnp.int32, (LANES, LANES), 0)

    def body(r, carry):
        levels_at = pl.ds(r, levels, stride=rows)
        t0_ref[0:levels] = st_ref[0, levels_at, :]
        t0_ref[HALF : HALF + levels] = st_ref[1, levels_at, :]
        t1_ref[0:levels] = zon_ref[levels_at, :]
        t1_ref[HALF : HALF + levels] = mer_ref[levels_at, :]
        t2_ref[0:levels] = mix_ref[levels_at, :]
        t2_ref[HALF:LANES] = jnp.broadcast_to(wet_ref[pl.ds(r, 1), :], (LANES - HALF, LANES))
        f0 = jnp.broadcast_to(flux_ref[0, pl.ds(r, 1), :], (LANES, LANES))
        f1 = jnp.broadcast_to(flux_ref[1, pl.ds(r, 1), :], (LANES, LANES))
        t0 = t0_ref[...]
        t0 = jnp.where(sub == levels, f0, t0)
        t0 = jnp.where(sub == HALF + levels, f1, t0)
        o_ref[r, :, 0:LANES] = jnp.transpose(t0)
        o_ref[r, :, LANES : 2 * LANES] = jnp.transpose(t1_ref[...])
        o_ref[r, :, 2 * LANES : 3 * LANES] = jnp.transpose(t2_ref[...])
        return carry

    for r in range(rows):
        body(r, 0)


def pack(tracers, zonal, meridional, mixing, wet, flux):
    fields, levels, rows, cols = tracers.shape
    return pl.pallas_call(
        functools.partial(pack_kernel, levels=levels),
        out_shape=jax.ShapeDtypeStruct((rows, cols, 3 * LANES), jnp.float32),
        scratch_shapes=[pltpu.VMEM((LANES, LANES), jnp.float32) for _ in range(3)],
        interpret=INTERPRET,
    )(
        tracers.reshape(fields, levels * rows, cols),
        zonal.reshape(levels * rows, cols),
        meridional.reshape(levels * rows, cols),
        mixing.reshape(levels * rows, cols),
        wet,
        flux,
    )


def to_lanes(x, fill):
    return jnp.concatenate([jnp.transpose(x, (1, 2, 0)), fill], axis=-1)


def shards(state, zonal, meridional, mixing, exchange_rate, sea_mask, regrid_map):
    tracers = state[0]
    fields, levels, rows, cols = tracers.shape
    section = lax.axis_index("sec")
    sea = sea_mask[0].astype(jnp.float32)
    wet = jnp.where(section == 1, sea, jnp.ones_like(sea))
    surface = jnp.stack([tracers[f, 0] for f in range(fields)])
    partner = lax.ppermute(surface, "sec", [(0, 1), (1, 0)])

    regridded = regrid(partner, regrid_map[0])
    flux = exchange_rate[0] * sea * (regridded - surface)

    x = pack(tracers, zonal[0], meridional[0], mixing[0], wet, flux)

    width = SUB
    row_block = lax.axis_index("lat")
    wet_lane = lax.broadcasted_iota(jnp.int32, (1, 1, 3 * LANES), 2) >= 2 * LANES + HALF
    top_mask = jnp.logical_and(wet_lane, row_block == 0)
    bot_mask = jnp.logical_and(wet_lane, row_block == lax.axis_size("lat") - 1)
    top = jnp.where(top_mask, 0.0, shifted(x[-width:], "lat", 1, cyclic=False))
    bot = jnp.where(bot_mask, 0.0, shifted(x[:width], "lat", -1, cyclic=False))
    left = shifted(x[:, -COL_PAD:], "lon", 1)
    right = shifted(x[:, :COL_PAD], "lon", -1)
    upper = jnp.where(top_mask, 0.0, shifted(jnp.concatenate([left[-width:], right[-width:]], axis=1), "lat", 1, cyclic=False))
    lower = jnp.where(bot_mask, 0.0, shifted(jnp.concatenate([left[:width], right[:width]], axis=1), "lat", -1, cyclic=False))
    left = jnp.concatenate([upper[:, :COL_PAD], left, lower[:, :COL_PAD]], axis=0)
    right = jnp.concatenate([upper[:, COL_PAD:], right, lower[:, COL_PAD:]], axis=0)

    out = run_steps(x, top, bot, left, right, levels, width)
    q = out.reshape(fields, levels, rows, cols)
    return (q[None], flux[None])


def solution(mesh):
    return jax.shard_map(
        shards,
        mesh=mesh,
        in_specs=(
            P("sec", None, None, "lat", "lon"),
            P("sec", None, "lat", "lon"),
            P("sec", None, "lat", "lon"),
            P("sec", None, "lat", "lon"),
            P("sec", "lat", "lon"),
            P("sec", "lat", "lon"),
            P("sec", None, "lat", "lon"),
        ),
        out_specs=(P("sec", None, None, "lat", "lon"), P("sec", None, "lat", "lon")),
        check_vma=False,
    )
```

```python
import functools

import jax
import jax.numpy as jnp
from jax import lax
from jax.experimental import pallas as pl
from jax.experimental.pallas import tpu as pltpu
from jax.sharding import PartitionSpec as P

TAPS = 4
SUB = 4
ROW_REACH = 2
COL_REACH = 3
LANES = 128
HALF = 64
COL_PAD = 8
INTERPRET = False


def shifted(x, axis, step, cyclic=True):
    count = lax.axis_size(axis)
    pairs = [(i, (i + step) % count) for i in range(count) if cyclic or 0 <= i + step < count]
    return lax.ppermute(x, axis, pairs)


def regrid(partner, table):
    fields, rows, cols = partner.shape
    row = lax.broadcasted_iota(jnp.int32, (rows, cols), 0)
    col = lax.broadcasted_iota(jnp.int32, (rows, cols), 1)
    d_row = table // cols - row
    d_col = table % cols - col
    d_col = jnp.where(d_col > cols // 2, d_col - cols, d_col)
    d_col = jnp.where(d_col < -(cols // 2), d_col + cols, d_col)
    padded = jnp.concatenate(
        [jnp.repeat(partner[:, :1], ROW_REACH, axis=1), partner, jnp.repeat(partner[:, -1:], ROW_REACH, axis=1)],
        axis=1,
    )
    moved = {}
    for a in range(-ROW_REACH, ROW_REACH + 1):
        rows_a = padded[:, ROW_REACH + a : ROW_REACH + a + rows]
        for b in range(-COL_REACH, COL_REACH + 1):
            moved[a, b] = jnp.roll(rows_a, -b, axis=2)
    total = None
    for tap in range(TAPS):
        picked = moved[0, 0]
        for (a, b), values in moved.items():
            hit = jnp.logical_and(d_row[tap] == a, d_col[tap] == b)
            picked = jnp.where(hit[None], values, picked)
        total = picked if total is None else total + picked
    return total / TAPS


def steps_kernel(x_ref, top_ref, bot_ref, left_ref, right_ref, o_ref,
                 s_ref, qa_ref, qb_ref, cw_ref, ce_ref, cs_ref, cn_ref, wc_ref, mx_ref, fl_ref, *, levels, width):
    rows, cols = x_ref.shape[0], x_ref.shape[1]
    ext_rows = rows + 2 * width
    ext_cols = cols + 2 * COL_PAD
    s_ref[width : width + rows, COL_PAD : COL_PAD + cols, :] = x_ref[...]
    s_ref[0:width, COL_PAD : COL_PAD + cols, :] = top_ref[...]
    s_ref[width + rows :, COL_PAD : COL_PAD + cols, :] = bot_ref[...]
    s_ref[:, 0:COL_PAD, :] = left_ref[...]
    s_ref[:, COL_PAD + cols :, :] = right_ref[...]

    lane = lax.broadcasted_iota(jnp.int32, (ext_cols, LANES), 1)
    low = lane < HALF
    level = lane % HALF
    down_ok = level < levels - 1
    level0 = level == 0

    def swap_halves(v):
        return pltpu.roll(v, HALF, 1)

    def wet_of(v):
        return jnp.where(low, swap_halves(v), v)

    def coef_row(r, carry):
        v1 = s_ref[r, :, LANES : 2 * LANES]
        v2 = s_ref[r, :, 2 * LANES : 3 * LANES]
        zon = jnp.where(low, v1, swap_halves(v1))
        mer = jnp.where(low, swap_halves(v1), v1)
        mix = jnp.where(low, v2, swap_halves(v2))
        wet_c = wet_of(v2)
        wet_s = wet_of(s_ref[r - 1, :, 2 * LANES : 3 * LANES])
        wet_n = wet_of(s_ref[r + 1, :, 2 * LANES : 3 * LANES])
        wet_w = pltpu.roll(wet_c, 1, 0)
        wet_e = pltpu.roll(wet_c, ext_cols - 1, 0)
        cw_ref[r] = wet_w * jnp.maximum(zon, 0.0)
        ce_ref[r] = wet_e * jnp.maximum(-zon, 0.0)
        cs_ref[r] = wet_s * jnp.maximum(mer, 0.0)
        cn_ref[r] = wet_n * jnp.maximum(-mer, 0.0)
        wc_ref[r] = wet_c
        mx_ref[r] = mix
        fl_ref[r] = pltpu.roll(s_ref[r, :, 0:LANES], LANES - levels, 1)
        return carry

    lax.fori_loop(1, ext_rows - 1, coef_row, 0)
    qa_ref[...] = s_ref[:, :, 0:LANES]

    def step(src, dst, k):
        def body(r, carry):
            qc = src[r]
            qs = src[r - 1]
            qn = src[r + 1]
            qw = pltpu.roll(qc, 1, 0)
            qe = pltpu.roll(qc, ext_cols - 1, 0)
            horiz = (
                cw_ref[r] * (qw - qc)
                + ce_ref[r] * (qe - qc)
                + cs_ref[r] * (qs - qc)
                + cn_ref[r] * (qn - qc)
            )
            up = pltpu.roll(qc, LANES - 1, 1)
            down = jnp.where(down_ok, mx_ref[r] * (up - qc), 0.0)
            vert = down - pltpu.roll(down, 1, 1)
            updated = qc + wc_ref[r] * (horiz + vert)
            dst[r] = jnp.where(level0, updated + fl_ref[r], updated)
            return carry

        lax.fori_loop(k + 1, ext_rows - 1 - k, body, 0)

    for k in range(SUB):
        if k % 2 == 0:
            step(qa_ref, qb_ref, k)
        else:
            step(qb_ref, qa_ref, k)
    final = qa_ref if SUB % 2 == 0 else qb_ref
    for r in range(rows):
        tile = jnp.transpose(final[width + r, COL_PAD : COL_PAD + cols, :])
        for f in range(o_ref.shape[0]):
            o_ref[f, pl.ds(r, levels, stride=rows), :] = tile[f * HALF : f * HALF + levels]


def run_steps(x, top, bot, left, right, levels, width):
    rows, cols, _ = x.shape
    ext = (rows + 2 * width, cols + 2 * COL_PAD, LANES)
    scratch = [pltpu.VMEM((rows + 2 * width, cols + 2 * COL_PAD, 3 * LANES), jnp.float32)]
    scratch += [pltpu.VMEM(ext, jnp.float32) for _ in range(9)]
    return pl.pallas_call(
        functools.partial(steps_kernel, levels=levels, width=width),
        out_shape=jax.ShapeDtypeStruct((LANES // HALF, levels * rows, cols), jnp.float32),
        scratch_shapes=scratch,
        compiler_params=pltpu.CompilerParams(vmem_limit_bytes=60 * 1024 * 1024),
        interpret=INTERPRET,
    )(x, top, bot, left, right)


def pack_kernel(st_ref, zon_ref, mer_ref, mix_ref, wet_ref, flux_ref, o_ref, last_ref, first_ref, east_ref, west_ref,
                t0_ref, t1_ref, t2_ref, *, levels, width):
    rows = wet_ref.shape[0]
    for t_ref in (t0_ref, t1_ref, t2_ref):
        t_ref[...] = jnp.zeros(t_ref.shape, jnp.float32)
    sub = lax.broadcasted_iota(jnp.int32, (LANES, LANES), 0)

    def body(r, carry):
        levels_at = pl.ds(r, levels, stride=rows)
        t0_ref[0:levels] = st_ref[0, levels_at, :]
        t0_ref[HALF : HALF + levels] = st_ref[1, levels_at, :]
        t1_ref[0:levels] = zon_ref[levels_at, :]
        t1_ref[HALF : HALF + levels] = mer_ref[levels_at, :]
        t2_ref[0:levels] = mix_ref[levels_at, :]
        t2_ref[HALF:LANES] = jnp.broadcast_to(wet_ref[pl.ds(r, 1), :], (LANES - HALF, LANES))
        f0 = jnp.broadcast_to(flux_ref[0, pl.ds(r, 1), :], (LANES, LANES))
        f1 = jnp.broadcast_to(flux_ref[1, pl.ds(r, 1), :], (LANES, LANES))
        t0 = t0_ref[...]
        t0 = jnp.where(sub == levels, f0, t0)
        t0 = jnp.where(sub == HALF + levels, f1, t0)
        for b, tile in enumerate((t0, t1_ref[...], t2_ref[...])):
            lanes = slice(b * LANES, (b + 1) * LANES)
            cell = jnp.transpose(tile)
            o_ref[r, :, lanes] = cell
            if r >= rows - width:
                last_ref[r - (rows - width), :, lanes] = cell
            if r < width:
                first_ref[r, :, lanes] = cell
            east_ref[r, :, lanes] = cell[-COL_PAD:]
            west_ref[r, :, lanes] = cell[:COL_PAD]
        return carry

    for r in range(rows):
        body(r, 0)


def pack(tracers, zonal, meridional, mixing, wet, flux, width):
    fields, levels, rows, cols = tracers.shape
    return pl.pallas_call(
        functools.partial(pack_kernel, levels=levels, width=width),
        out_shape=(
            jax.ShapeDtypeStruct((rows, cols, 3 * LANES), jnp.float32),
            jax.ShapeDtypeStruct((width, cols, 3 * LANES), jnp.float32),
            jax.ShapeDtypeStruct((width, cols, 3 * LANES), jnp.float32),
            jax.ShapeDtypeStruct((rows, COL_PAD, 3 * LANES), jnp.float32),
            jax.ShapeDtypeStruct((rows, COL_PAD, 3 * LANES), jnp.float32),
        ),
        scratch_shapes=[pltpu.VMEM((LANES, LANES), jnp.float32) for _ in range(3)],
        interpret=INTERPRET,
    )(
        tracers.reshape(fields, levels * rows, cols),
        zonal.reshape(levels * rows, cols),
        meridional.reshape(levels * rows, cols),
        mixing.reshape(levels * rows, cols),
        wet,
        flux,
    )


def to_lanes(x, fill):
    return jnp.concatenate([jnp.transpose(x, (1, 2, 0)), fill], axis=-1)


def shards(state, zonal, meridional, mixing, exchange_rate, sea_mask, regrid_map):
    tracers = state[0]
    fields, levels, rows, cols = tracers.shape
    section = lax.axis_index("sec")
    sea = sea_mask[0].astype(jnp.float32)
    wet = jnp.where(section == 1, sea, jnp.ones_like(sea))
    surface = jnp.stack([tracers[f, 0] for f in range(fields)])
    partner = lax.ppermute(surface, "sec", [(0, 1), (1, 0)])

    regridded = regrid(partner, regrid_map[0])
    flux = exchange_rate[0] * sea * (regridded - surface)

    x, last, first, east, west = pack(tracers, zonal[0], meridional[0], mixing[0], wet, flux, SUB)

    width = SUB
    row_block = lax.axis_index("lat")
    wet_lane = lax.broadcasted_iota(jnp.int32, (1, 1, 3 * LANES), 2) >= 2 * LANES + HALF
    top_mask = jnp.logical_and(wet_lane, row_block == 0)
    bot_mask = jnp.logical_and(wet_lane, row_block == lax.axis_size("lat") - 1)
    top = jnp.where(top_mask, 0.0, shifted(last, "lat", 1, cyclic=False))
    bot = jnp.where(bot_mask, 0.0, shifted(first, "lat", -1, cyclic=False))
    left = shifted(east, "lon", 1)
    right = shifted(west, "lon", -1)
    upper = jnp.where(top_mask, 0.0, shifted(jnp.concatenate([left[-width:], right[-width:]], axis=1), "lat", 1, cyclic=False))
    lower = jnp.where(bot_mask, 0.0, shifted(jnp.concatenate([left[:width], right[:width]], axis=1), "lat", -1, cyclic=False))
    left = jnp.concatenate([upper[:, :COL_PAD], left, lower[:, :COL_PAD]], axis=0)
    right = jnp.concatenate([upper[:, COL_PAD:], right, lower[:, COL_PAD:]], axis=0)

    out = run_steps(x, top, bot, left, right, levels, width)
    q = out.reshape(fields, levels, rows, cols)
    return (q[None], flux[None])


def solution(mesh):
    return jax.shard_map(
        shards,
        mesh=mesh,
        in_specs=(
            P("sec", None, None, "lat", "lon"),
            P("sec", None, "lat", "lon"),
            P("sec", None, "lat", "lon"),
            P("sec", None, "lat", "lon"),
            P("sec", "lat", "lon"),
            P("sec", "lat", "lon"),
            P("sec", None, "lat", "lon"),
        ),
        out_specs=(P("sec", None, None, "lat", "lon"), P("sec", None, "lat", "lon")),
        check_vma=False,
    )
```

```python
import functools

import jax
import jax.numpy as jnp
from jax import lax
from jax.experimental import pallas as pl
from jax.experimental.pallas import tpu as pltpu
from jax.sharding import PartitionSpec as P

TAPS = 4
SUB = 4
ROW_REACH = 2
COL_REACH = 3
LANES = 128
HALF = 64
COL_PAD = 8
INTERPRET = False


def shifted(x, axis, step, cyclic=True):
    count = lax.axis_size(axis)
    pairs = [(i, (i + step) % count) for i in range(count) if cyclic or 0 <= i + step < count]
    return lax.ppermute(x, axis, pairs)


def regrid(partner, table):
    fields, rows, cols = partner.shape
    row = lax.broadcasted_iota(jnp.int32, (rows, cols), 0)
    col = lax.broadcasted_iota(jnp.int32, (rows, cols), 1)
    d_row = table // cols - row
    d_col = table % cols - col
    d_col = jnp.where(d_col > cols // 2, d_col - cols, d_col)
    d_col = jnp.where(d_col < -(cols // 2), d_col + cols, d_col)
    padded = jnp.concatenate(
        [jnp.repeat(partner[:, :1], ROW_REACH, axis=1), partner, jnp.repeat(partner[:, -1:], ROW_REACH, axis=1)],
        axis=1,
    )
    moved = {}
    for a in range(-ROW_REACH, ROW_REACH + 1):
        rows_a = padded[:, ROW_REACH + a : ROW_REACH + a + rows]
        for b in range(-COL_REACH, COL_REACH + 1):
            moved[a, b] = jnp.roll(rows_a, -b, axis=2)
    total = None
    for tap in range(TAPS):
        picked = moved[0, 0]
        for (a, b), values in moved.items():
            hit = jnp.logical_and(d_row[tap] == a, d_col[tap] == b)
            picked = jnp.where(hit[None], values, picked)
        total = picked if total is None else total + picked
    return total / TAPS


def steps_kernel(x_ref, top_ref, bot_ref, left_ref, right_ref, o_ref,
                 s_ref, qa_ref, qb_ref, cw_ref, ce_ref, cs_ref, cn_ref, wc_ref, mx_ref, fl_ref, *, levels, width):
    rows, cols = x_ref.shape[0], x_ref.shape[1]
    ext_rows = rows + 2 * width
    ext_cols = cols + 2 * COL_PAD
    s_ref[width : width + rows, COL_PAD : COL_PAD + cols, :] = x_ref[...]
    s_ref[0:width, COL_PAD : COL_PAD + cols, :] = top_ref[...]
    s_ref[width + rows :, COL_PAD : COL_PAD + cols, :] = bot_ref[...]
    s_ref[:, 0:COL_PAD, :] = left_ref[...]
    s_ref[:, COL_PAD + cols :, :] = right_ref[...]

    lane = lax.broadcasted_iota(jnp.int32, (ext_cols, LANES), 1)
    low = lane < HALF
    level = lane % HALF
    down_ok = level < levels - 1
    level0 = level == 0

    def swap_halves(v):
        return pltpu.roll(v, HALF, 1)

    def wet_of(v):
        return jnp.where(low, swap_halves(v), v)

    def coef_row(r, carry):
        v1 = s_ref[r, :, LANES : 2 * LANES]
        v2 = s_ref[r, :, 2 * LANES : 3 * LANES]
        zon = jnp.where(low, v1, swap_halves(v1))
        mer = jnp.where(low, swap_halves(v1), v1)
        mix = jnp.where(low, v2, swap_halves(v2))
        wet_c = wet_of(v2)
        wet_s = wet_of(s_ref[r - 1, :, 2 * LANES : 3 * LANES])
        wet_n = wet_of(s_ref[r + 1, :, 2 * LANES : 3 * LANES])
        wet_w = pltpu.roll(wet_c, 1, 0)
        wet_e = pltpu.roll(wet_c, ext_cols - 1, 0)
        cw_ref[r] = wet_w * jnp.maximum(zon, 0.0)
        ce_ref[r] = wet_e * jnp.maximum(-zon, 0.0)
        cs_ref[r] = wet_s * jnp.maximum(mer, 0.0)
        cn_ref[r] = wet_n * jnp.maximum(-mer, 0.0)
        wc_ref[r] = wet_c
        mx_ref[r] = mix
        fl_ref[r] = pltpu.roll(s_ref[r, :, 0:LANES], LANES - levels, 1)
        return carry

    lax.fori_loop(1, ext_rows - 1, coef_row, 0)
    qa_ref[...] = s_ref[:, :, 0:LANES]

    def step(src, dst, k):
        def body(r, carry):
            qc = src[r]
            qs = src[r - 1]
            qn = src[r + 1]
            qw = pltpu.roll(qc, 1, 0)
            qe = pltpu.roll(qc, ext_cols - 1, 0)
            horiz = (
                cw_ref[r] * (qw - qc)
                + ce_ref[r] * (qe - qc)
                + cs_ref[r] * (qs - qc)
                + cn_ref[r] * (qn - qc)
            )
            up = pltpu.roll(qc, LANES - 1, 1)
            down = jnp.where(down_ok, mx_ref[r] * (up - qc), 0.0)
            vert = down - pltpu.roll(down, 1, 1)
            updated = qc + wc_ref[r] * (horiz + vert)
            dst[r] = jnp.where(level0, updated + fl_ref[r], updated)
            return carry

        lax.fori_loop(k + 1, ext_rows - 1 - k, body, 0, unroll=2)

    for k in range(SUB):
        if k % 2 == 0:
            step(qa_ref, qb_ref, k)
        else:
            step(qb_ref, qa_ref, k)
    final = qa_ref if SUB % 2 == 0 else qb_ref
    for r in range(rows):
        tile = jnp.transpose(final[width + r, COL_PAD : COL_PAD + cols, :])
        for f in range(o_ref.shape[0]):
            o_ref[f, pl.ds(r, levels, stride=rows), :] = tile[f * HALF : f * HALF + levels]


def run_steps(x, top, bot, left, right, levels, width):
    rows, cols, _ = x.shape
    ext = (rows + 2 * width, cols + 2 * COL_PAD, LANES)
    scratch = [pltpu.VMEM((rows + 2 * width, cols + 2 * COL_PAD, 3 * LANES), jnp.float32)]
    scratch += [pltpu.VMEM(ext, jnp.float32) for _ in range(9)]
    return pl.pallas_call(
        functools.partial(steps_kernel, levels=levels, width=width),
        out_shape=jax.ShapeDtypeStruct((LANES // HALF, levels * rows, cols), jnp.float32),
        scratch_shapes=scratch,
        compiler_params=pltpu.CompilerParams(vmem_limit_bytes=60 * 1024 * 1024),
        interpret=INTERPRET,
    )(x, top, bot, left, right)


def pack_kernel(st_ref, zon_ref, mer_ref, mix_ref, wet_ref, flux_ref, o_ref, t0_ref, t1_ref, t2_ref, *, levels):
    rows = wet_ref.shape[0]
    for t_ref in (t0_ref, t1_ref, t2_ref):
        t_ref[...] = jnp.zeros(t_ref.shape, jnp.float32)
    sub = lax.broadcasted_iota(jnp.int32, (LANES, LANES), 0)

    def body(r, carry):
        levels_at = pl.ds(r, levels, stride=rows)
        t0_ref[0:levels] = st_ref[0, levels_at, :]
        t0_ref[HALF : HALF + levels] = st_ref[1, levels_at, :]
        t1_ref[0:levels] = zon_ref[levels_at, :]
        t1_ref[HALF : HALF + levels] = mer_ref[levels_at, :]
        t2_ref[0:levels] = mix_ref[levels_at, :]
        t2_ref[HALF:LANES] = jnp.broadcast_to(wet_ref[pl.ds(r, 1), :], (LANES - HALF, LANES))
        f0 = jnp.broadcast_to(flux_ref[0, pl.ds(r, 1), :], (LANES, LANES))
        f1 = jnp.broadcast_to(flux_ref[1, pl.ds(r, 1), :], (LANES, LANES))
        t0 = t0_ref[...]
        t0 = jnp.where(sub == levels, f0, t0)
        t0 = jnp.where(sub == HALF + levels, f1, t0)
        o_ref[r, :, 0:LANES] = jnp.transpose(t0)
        o_ref[r, :, LANES : 2 * LANES] = jnp.transpose(t1_ref[...])
        o_ref[r, :, 2 * LANES : 3 * LANES] = jnp.transpose(t2_ref[...])
        return carry

    for r in range(rows):
        body(r, 0)


def pack(tracers, zonal, meridional, mixing, wet, flux):
    fields, levels, rows, cols = tracers.shape
    return pl.pallas_call(
        functools.partial(pack_kernel, levels=levels),
        out_shape=jax.ShapeDtypeStruct((rows, cols, 3 * LANES), jnp.float32),
        scratch_shapes=[pltpu.VMEM((LANES, LANES), jnp.float32) for _ in range(3)],
        interpret=INTERPRET,
    )(
        tracers.reshape(fields, levels * rows, cols),
        zonal.reshape(levels * rows, cols),
        meridional.reshape(levels * rows, cols),
        mixing.reshape(levels * rows, cols),
        wet,
        flux,
    )


def to_lanes(x, fill):
    return jnp.concatenate([jnp.transpose(x, (1, 2, 0)), fill], axis=-1)


def shards(state, zonal, meridional, mixing, exchange_rate, sea_mask, regrid_map):
    tracers = state[0]
    fields, levels, rows, cols = tracers.shape
    section = lax.axis_index("sec")
    sea = sea_mask[0].astype(jnp.float32)
    wet = jnp.where(section == 1, sea, jnp.ones_like(sea))
    surface = jnp.stack([tracers[f, 0] for f in range(fields)])
    partner = lax.ppermute(surface, "sec", [(0, 1), (1, 0)])

    regridded = regrid(partner, regrid_map[0])
    flux = exchange_rate[0] * sea * (regridded - surface)

    x = pack(tracers, zonal[0], meridional[0], mixing[0], wet, flux)

    width = SUB
    row_block = lax.axis_index("lat")
    wet_lane = lax.broadcasted_iota(jnp.int32, (1, 1, 3 * LANES), 2) >= 2 * LANES + HALF
    top_mask = jnp.logical_and(wet_lane, row_block == 0)
    bot_mask = jnp.logical_and(wet_lane, row_block == lax.axis_size("lat") - 1)
    top = jnp.where(top_mask, 0.0, shifted(x[-width:], "lat", 1, cyclic=False))
    bot = jnp.where(bot_mask, 0.0, shifted(x[:width], "lat", -1, cyclic=False))
    left = shifted(x[:, -COL_PAD:], "lon", 1)
    right = shifted(x[:, :COL_PAD], "lon", -1)
    upper = jnp.where(top_mask, 0.0, shifted(jnp.concatenate([left[-width:], right[-width:]], axis=1), "lat", 1, cyclic=False))
    lower = jnp.where(bot_mask, 0.0, shifted(jnp.concatenate([left[:width], right[:width]], axis=1), "lat", -1, cyclic=False))
    left = jnp.concatenate([upper[:, :COL_PAD], left, lower[:, :COL_PAD]], axis=0)
    right = jnp.concatenate([upper[:, COL_PAD:], right, lower[:, COL_PAD:]], axis=0)

    out = run_steps(x, top, bot, left, right, levels, width)
    q = out.reshape(fields, levels, rows, cols)
    return (q[None], flux[None])


def solution(mesh):
    return jax.shard_map(
        shards,
        mesh=mesh,
        in_specs=(
            P("sec", None, None, "lat", "lon"),
            P("sec", None, "lat", "lon"),
            P("sec", None, "lat", "lon"),
            P("sec", None, "lat", "lon"),
            P("sec", "lat", "lon"),
            P("sec", "lat", "lon"),
            P("sec", None, "lat", "lon"),
        ),
        out_specs=(P("sec", None, None, "lat", "lon"), P("sec", None, "lat", "lon")),
        check_vma=False,
    )
```

```python
import functools

import jax
import jax.numpy as jnp
from jax import lax
from jax.experimental import pallas as pl
from jax.experimental.pallas import tpu as pltpu
from jax.sharding import PartitionSpec as P

TAPS = 4
SUB = 4
ROW_REACH = 2
COL_REACH = 3
LANES = 128
HALF = 64
COL_PAD = 8
INTERPRET = False


def shifted(x, axis, step, cyclic=True):
    count = lax.axis_size(axis)
    pairs = [(i, (i + step) % count) for i in range(count) if cyclic or 0 <= i + step < count]
    return lax.ppermute(x, axis, pairs)


def regrid(partner, table):
    fields, rows, cols = partner.shape
    row = lax.broadcasted_iota(jnp.int32, (rows, cols), 0)
    col = lax.broadcasted_iota(jnp.int32, (rows, cols), 1)
    d_row = table // cols - row
    d_col = table % cols - col
    d_col = jnp.where(d_col > cols // 2, d_col - cols, d_col)
    d_col = jnp.where(d_col < -(cols // 2), d_col + cols, d_col)
    padded = jnp.concatenate(
        [jnp.repeat(partner[:, :1], ROW_REACH, axis=1), partner, jnp.repeat(partner[:, -1:], ROW_REACH, axis=1)],
        axis=1,
    )
    moved = {}
    for a in range(-ROW_REACH, ROW_REACH + 1):
        rows_a = padded[:, ROW_REACH + a : ROW_REACH + a + rows]
        for b in range(-COL_REACH, COL_REACH + 1):
            moved[a, b] = jnp.roll(rows_a, -b, axis=2)
    total = None
    for tap in range(TAPS):
        picked = moved[0, 0]
        for (a, b), values in moved.items():
            hit = jnp.logical_and(d_row[tap] == a, d_col[tap] == b)
            picked = jnp.where(hit[None], values, picked)
        total = picked if total is None else total + picked
    return total / TAPS


def steps_kernel(x_ref, top_ref, bot_ref, left_ref, right_ref, o_ref,
                 s_ref, qa_ref, qb_ref, cw_ref, ce_ref, cs_ref, cn_ref, wc_ref, mx_ref, fl_ref, *, levels, width):
    rows, cols = x_ref.shape[0], x_ref.shape[1]
    ext_rows = rows + 2 * width
    ext_cols = cols + 2 * COL_PAD
    s_ref[width : width + rows, COL_PAD : COL_PAD + cols, :] = x_ref[...]
    s_ref[0:width, COL_PAD : COL_PAD + cols, :] = top_ref[...]
    s_ref[width + rows :, COL_PAD : COL_PAD + cols, :] = bot_ref[...]
    s_ref[:, 0:COL_PAD, :] = left_ref[...]
    s_ref[:, COL_PAD + cols :, :] = right_ref[...]

    lane = lax.broadcasted_iota(jnp.int32, (ext_cols, LANES), 1)
    low = lane < HALF
    level = lane % HALF
    down_ok = level < levels - 1
    level0 = level == 0

    def swap_halves(v):
        return pltpu.roll(v, HALF, 1)

    def wet_of(v):
        return jnp.where(low, swap_halves(v), v)

    def coef_row(r, carry):
        v1 = s_ref[r, :, LANES : 2 * LANES]
        v2 = s_ref[r, :, 2 * LANES : 3 * LANES]
        zon = jnp.where(low, v1, swap_halves(v1))
        mer = jnp.where(low, swap_halves(v1), v1)
        mix = jnp.where(low, v2, swap_halves(v2))
        wet_c = wet_of(v2)
        wet_s = wet_of(s_ref[r - 1, :, 2 * LANES : 3 * LANES])
        wet_n = wet_of(s_ref[r + 1, :, 2 * LANES : 3 * LANES])
        wet_w = pltpu.roll(wet_c, 1, 0)
        wet_e = pltpu.roll(wet_c, ext_cols - 1, 0)
        cw_ref[r] = wet_w * jnp.maximum(zon, 0.0)
        ce_ref[r] = wet_e * jnp.maximum(-zon, 0.0)
        cs_ref[r] = wet_s * jnp.maximum(mer, 0.0)
        cn_ref[r] = wet_n * jnp.maximum(-mer, 0.0)
        wc_ref[r] = wet_c
        mx_ref[r] = mix
        fl_ref[r] = pltpu.roll(s_ref[r, :, 0:LANES], LANES - levels, 1)
        return carry

    lax.fori_loop(1, ext_rows - 1, coef_row, 0)
    qa_ref[...] = s_ref[:, :, 0:LANES]

    def step(src, dst, k):
        def body(r, carry):
            qc = src[r]
            qs = src[r - 1]
            qn = src[r + 1]
            qw = pltpu.roll(qc, 1, 0)
            qe = pltpu.roll(qc, ext_cols - 1, 0)
            horiz = (
                cw_ref[r] * (qw - qc)
                + ce_ref[r] * (qe - qc)
                + cs_ref[r] * (qs - qc)
                + cn_ref[r] * (qn - qc)
            )
            up = pltpu.roll(qc, LANES - 1, 1)
            down = jnp.where(down_ok, mx_ref[r] * (up - qc), 0.0)
            vert = down - pltpu.roll(down, 1, 1)
            updated = qc + wc_ref[r] * (horiz + vert)
            dst[r] = jnp.where(level0, updated + fl_ref[r], updated)
            return carry

        lax.fori_loop(k + 1, ext_rows - 1 - k, body, 0, unroll=4)

    for k in range(SUB):
        if k % 2 == 0:
            step(qa_ref, qb_ref, k)
        else:
            step(qb_ref, qa_ref, k)
    final = qa_ref if SUB % 2 == 0 else qb_ref
    for r in range(rows):
        tile = jnp.transpose(final[width + r, COL_PAD : COL_PAD + cols, :])
        for f in range(o_ref.shape[0]):
            o_ref[f, pl.ds(r, levels, stride=rows), :] = tile[f * HALF : f * HALF + levels]


def run_steps(x, top, bot, left, right, levels, width):
    rows, cols, _ = x.shape
    ext = (rows + 2 * width, cols + 2 * COL_PAD, LANES)
    scratch = [pltpu.VMEM((rows + 2 * width, cols + 2 * COL_PAD, 3 * LANES), jnp.float32)]
    scratch += [pltpu.VMEM(ext, jnp.float32) for _ in range(9)]
    return pl.pallas_call(
        functools.partial(steps_kernel, levels=levels, width=width),
        out_shape=jax.ShapeDtypeStruct((LANES // HALF, levels * rows, cols), jnp.float32),
        scratch_shapes=scratch,
        compiler_params=pltpu.CompilerParams(vmem_limit_bytes=60 * 1024 * 1024),
        interpret=INTERPRET,
    )(x, top, bot, left, right)


def pack_kernel(st_ref, zon_ref, mer_ref, mix_ref, wet_ref, flux_ref, o_ref, t0_ref, t1_ref, t2_ref, *, levels):
    rows = wet_ref.shape[0]
    for t_ref in (t0_ref, t1_ref, t2_ref):
        t_ref[...] = jnp.zeros(t_ref.shape, jnp.float32)
    sub = lax.broadcasted_iota(jnp.int32, (LANES, LANES), 0)

    def body(r, carry):
        levels_at = pl.ds(r, levels, stride=rows)
        t0_ref[0:levels] = st_ref[0, levels_at, :]
        t0_ref[HALF : HALF + levels] = st_ref[1, levels_at, :]
        t1_ref[0:levels] = zon_ref[levels_at, :]
        t1_ref[HALF : HALF + levels] = mer_ref[levels_at, :]
        t2_ref[0:levels] = mix_ref[levels_at, :]
        t2_ref[HALF:LANES] = jnp.broadcast_to(wet_ref[pl.ds(r, 1), :], (LANES - HALF, LANES))
        f0 = jnp.broadcast_to(flux_ref[0, pl.ds(r, 1), :], (LANES, LANES))
        f1 = jnp.broadcast_to(flux_ref[1, pl.ds(r, 1), :], (LANES, LANES))
        t0 = t0_ref[...]
        t0 = jnp.where(sub == levels, f0, t0)
        t0 = jnp.where(sub == HALF + levels, f1, t0)
        o_ref[r, :, 0:LANES] = jnp.transpose(t0)
        o_ref[r, :, LANES : 2 * LANES] = jnp.transpose(t1_ref[...])
        o_ref[r, :, 2 * LANES : 3 * LANES] = jnp.transpose(t2_ref[...])
        return carry

    for r in range(rows):
        body(r, 0)


def pack(tracers, zonal, meridional, mixing, wet, flux):
    fields, levels, rows, cols = tracers.shape
    return pl.pallas_call(
        functools.partial(pack_kernel, levels=levels),
        out_shape=jax.ShapeDtypeStruct((rows, cols, 3 * LANES), jnp.float32),
        scratch_shapes=[pltpu.VMEM((LANES, LANES), jnp.float32) for _ in range(3)],
        interpret=INTERPRET,
    )(
        tracers.reshape(fields, levels * rows, cols),
        zonal.reshape(levels * rows, cols),
        meridional.reshape(levels * rows, cols),
        mixing.reshape(levels * rows, cols),
        wet,
        flux,
    )


def to_lanes(x, fill):
    return jnp.concatenate([jnp.transpose(x, (1, 2, 0)), fill], axis=-1)


def shards(state, zonal, meridional, mixing, exchange_rate, sea_mask, regrid_map):
    tracers = state[0]
    fields, levels, rows, cols = tracers.shape
    section = lax.axis_index("sec")
    sea = sea_mask[0].astype(jnp.float32)
    wet = jnp.where(section == 1, sea, jnp.ones_like(sea))
    surface = jnp.stack([tracers[f, 0] for f in range(fields)])
    partner = lax.ppermute(surface, "sec", [(0, 1), (1, 0)])

    regridded = regrid(partner, regrid_map[0])
    flux = exchange_rate[0] * sea * (regridded - surface)

    x = pack(tracers, zonal[0], meridional[0], mixing[0], wet, flux)

    width = SUB
    row_block = lax.axis_index("lat")
    wet_lane = lax.broadcasted_iota(jnp.int32, (1, 1, 3 * LANES), 2) >= 2 * LANES + HALF
    top_mask = jnp.logical_and(wet_lane, row_block == 0)
    bot_mask = jnp.logical_and(wet_lane, row_block == lax.axis_size("lat") - 1)
    top = jnp.where(top_mask, 0.0, shifted(x[-width:], "lat", 1, cyclic=False))
    bot = jnp.where(bot_mask, 0.0, shifted(x[:width], "lat", -1, cyclic=False))
    left = shifted(x[:, -COL_PAD:], "lon", 1)
    right = shifted(x[:, :COL_PAD], "lon", -1)
    upper = jnp.where(top_mask, 0.0, shifted(jnp.concatenate([left[-width:], right[-width:]], axis=1), "lat", 1, cyclic=False))
    lower = jnp.where(bot_mask, 0.0, shifted(jnp.concatenate([left[:width], right[:width]], axis=1), "lat", -1, cyclic=False))
    left = jnp.concatenate([upper[:, :COL_PAD], left, lower[:, :COL_PAD]], axis=0)
    right = jnp.concatenate([upper[:, COL_PAD:], right, lower[:, COL_PAD:]], axis=0)

    out = run_steps(x, top, bot, left, right, levels, width)
    q = out.reshape(fields, levels, rows, cols)
    return (q[None], flux[None])


def solution(mesh):
    return jax.shard_map(
        shards,
        mesh=mesh,
        in_specs=(
            P("sec", None, None, "lat", "lon"),
            P("sec", None, "lat", "lon"),
            P("sec", None, "lat", "lon"),
            P("sec", None, "lat", "lon"),
            P("sec", "lat", "lon"),
            P("sec", "lat", "lon"),
            P("sec", None, "lat", "lon"),
        ),
        out_specs=(P("sec", None, None, "lat", "lon"), P("sec", None, "lat", "lon")),
        check_vma=False,
    )
```
